32 devices in a mesh: vert: 16 (over z, y, x), eig: 2 (over core).
Axes of the slice: x: 2, y: 2, z: 4, core: 2. Of those that a mesh axis runs over, the one named last changes fastest.
Arguments:
- eig_table: bfloat16 [32768, 2048], P('vert', 'eig'), may hold values from -0.1875 to 0.1875
- obs_ids: int32 [49152], P('vert'), may hold values from 0 to 2047
- counts: int32 [16], P('vert'), may hold values from 512 to 3072, as said below
- noise_var: float32 [49152], P('vert'), may hold values from 0.05 to 0.5
- eigenvalues: float32 [2048], P('eig'), may hold values from 0.01 to 4
- rhs: float32 [256, 49152], P('eig', 'vert'), may hold values from -6 to 6
Outputs:
- solution: float32 [256, 49152], P('eig', 'vert')
- residual: float32 [256, 49152], P('eig', 'vert')
The draws below stay inside these ranges and needn't reach their ends.
Inputs may be any that keep to these rules, and one draw needn't show every extreme that they name: `counts`: slots of a shard are filled from its first slot on; the busiest shard fills all 3072.
All inputs are finite; a program needn't handle non-finite values.
Results may differ from the reference program's by a relative error of at most 0.039.
Values may be sent and summed in bfloat16 or wider, within the bound.
No kernel may reach another device: no remote copies, remote signals or barrier semaphores. Data moves between devices by JAX's collectives and lax.ppermute only.
A program may use at most 64 MiB of HBM per device.

```python
import math
import jax
import jax.numpy as jnp
from jax import lax

M = 2048
SAMPLES = 256
CAP = 3072
LOCAL_V = 2048
ITERS = 2
NOBS = 49152
VERTS = 32768
EIG_DEV = 1024
N_VERT = 16
N_EIG = 2


def draw_counts(key, part):
    first_key, second_key = jax.random.split(key)
    divisor = jax.random.randint(first_key, (N_VERT,), 1, 7)
    filled = CAP // divisor
    busiest = jax.random.randint(second_key, (), 0, N_VERT)
    return jnp.where(jnp.arange(N_VERT) == busiest, CAP, filled).astype(jnp.int32)


def plant(entries, own_key, least, high):
    shape = entries.shape
    place = [jax.random.randint(jax.random.fold_in(own_key, axis), (), 0, shape[axis]) for axis in range(len(shape))]
    entries = entries.at[tuple(place)].set(least)
    longest = shape.index(max(shape))
    place[longest] = (place[longest] + 1) % shape[longest]
    return entries.at[tuple(place)].set(high)


def block_levels(stream_key, dims, shards, least, largest):
    loudness = 1.0
    for dim, parts in shards:
        heights = jax.random.uniform(jax.random.fold_in(jax.random.fold_in(stream_key, 6), dim), (parts,), jnp.float32, least / len(shards), largest / len(shards))
        loudness = loudness * jnp.repeat(jnp.exp(heights), dims[dim] // parts).reshape((-1,) + (1,) * (len(dims) - 1 - dim))
    return loudness


def scatter_about(own_key, extent, deviation, limit, cuts=(), kind=jnp.bfloat16):
    factor_of = block_levels(own_key, extent, cuts, -0.22, 0.18) if cuts else 1.0
    array = jax.random.normal(own_key, extent, jnp.float32) * deviation * factor_of
    return jnp.minimum(jnp.maximum(array, -limit), limit).astype(kind)


def setup_inputs(seed: int = 0) -> dict:
    keys = jax.random.split(jax.random.key(seed), 7)
    eig_table = scatter_about(keys[0], (VERTS, M), (M // 2) ** -0.5, 0.1875, ((0, 16), (1, 2)))
    obs_ids = plant(jax.random.randint(keys[1], (NOBS,), 0, LOCAL_V), jax.random.fold_in(keys[1], 1), 0, LOCAL_V - 1).astype(jnp.int32)
    counts = draw_counts(jax.random.fold_in(keys[6], 71), 0)
    noise_var = jnp.clip(jnp.exp(math.log(0.5) - 2.3025851 * jax.random.uniform(keys[3], (NOBS,), jnp.float32) ** block_levels(keys[3], (NOBS,), ((0, 16),), -0.2, 0.2)), 0.05, 0.5)
    eigenvalues = jnp.clip(jnp.exp(math.log(4.0) - 5.9914646 * jax.random.uniform(keys[4], (M,), jnp.float32) ** block_levels(keys[4], (M,), ((0, 2),), -0.2, 0.2)), 0.01, 4.0)
    rhs = scatter_about(keys[5], (SAMPLES, NOBS), 1.0, 6.0, ((0, 2), (1, 16)), jnp.float32)
    return {"eig_table": eig_table, "obs_ids": obs_ids, "counts": counts, "noise_var": noise_var, "eigenvalues": eigenvalues, "rhs": rhs}


def feature_rows(table_block, id_block, filled_block):
    picked = jnp.take(table_block, id_block, axis=0)
    return jnp.where(filled_block[:, None], picked, jnp.zeros((), jnp.bfloat16))


def reference(eig_table, obs_ids, counts, noise_var, eigenvalues, rhs):
    tables = eig_table.reshape(N_VERT, LOCAL_V, M)
    id_blocks = obs_ids.reshape(N_VERT, CAP)
    filled = jnp.arange(CAP, dtype=jnp.int32)[None, :] < counts[:, None]
    spectrum = 5.0 * jnp.power(3.0 + eigenvalues, -1.5)

    def operate(vector):
        lowered = vector.astype(jnp.bfloat16).reshape(SAMPLES, N_VERT, CAP).transpose(1, 0, 2)

        def accumulate(summed, blocks):
            table_block, id_block, filled_block, vector_block = blocks
            features = feature_rows(table_block, id_block, filled_block)
            return summed + jnp.dot(vector_block, features, preferred_element_type=jnp.float32), None

        coeff, unused = lax.scan(accumulate, jnp.zeros((SAMPLES, M), jnp.float32), (tables, id_blocks, filled, lowered))
        weights = (coeff * spectrum[None, :]).astype(jnp.bfloat16)
        grouped = weights.reshape(SAMPLES, N_EIG, EIG_DEV).astype(jnp.float32)

        def image_block(blocks):
            table_block, id_block, filled_block = blocks
            features = feature_rows(table_block, id_block, filled_block).reshape(CAP, N_EIG, EIG_DEV).astype(jnp.float32)
            partials = jnp.einsum("sge,cge->gsc", grouped, features)
            partials = lax.optimization_barrier(partials.astype(jnp.bfloat16)).astype(jnp.float32)
            return jnp.sum(partials, axis=0)

        applied = lax.map(image_block, (tables, id_blocks, filled))
        applied = applied.transpose(1, 0, 2).reshape(SAMPLES, NOBS)
        return applied + noise_var[None, :] * vector

    residual = jnp.where(filled.reshape(NOBS)[None, :], rhs, jnp.zeros((), jnp.float32))
    solution = jnp.zeros_like(residual)
    direction = residual
    norm_now = jnp.sum(residual * residual, axis=1)
    for iteration in range(ITERS):
        applied = operate(direction)
        step_size = norm_now / jnp.sum(direction * applied, axis=1)
        solution = solution + step_size[:, None] * direction
        residual = residual - step_size[:, None] * applied
        norm_next = jnp.sum(residual * residual, axis=1)
        direction = residual + (norm_next / norm_now)[:, None] * direction
        norm_now = norm_next
    return solution, residual
```

```python
import jax
import jax.numpy as jnp
from jax import lax
from jax.sharding import PartitionSpec as P

ITERS = 2


def butterfly(x, n_vert, finish):
    bits = n_vert.bit_length() - 1
    me = lax.axis_index("vert")
    cur = x
    for b in range(bits):
        half = cur.shape[1] // 2
        perm = [(i, i ^ (1 << b)) for i in range(n_vert)]
        upper = (me >> b) & 1
        keep = lax.dynamic_slice_in_dim(cur, upper * half, half, axis=1)
        send = lax.dynamic_slice_in_dim(cur, (1 - upper) * half, half, axis=1)
        cur = keep + lax.ppermute(send, "vert", perm)
    cur = finish(cur)
    for b in reversed(range(bits)):
        perm = [(i, i ^ (1 << b)) for i in range(n_vert)]
        upper = (me >> b) & 1
        got = lax.ppermute(cur, "vert", perm)
        cur = jnp.where(upper == 0, jnp.concatenate([cur, got], 1), jnp.concatenate([got, cur], 1))
    return cur


def make_shards(n_vert, n_eig):
    def shards(eig_table, obs_ids, counts, noise_var, eigenvalues, rhs):
        capacity = obs_ids.shape[0]
        own = rhs.shape[0]
        samples = own * n_eig
        group = eig_table.shape[1]
        filled = jnp.arange(capacity, dtype=jnp.int32) < counts[0]
        features = jnp.where(
            filled[:, None], jnp.take(eig_table, obs_ids, axis=0), jnp.zeros((), jnp.bfloat16)
        )
        spectrum = 5.0 * jnp.power(3.0 + eigenvalues, -1.5)
        me_eig = lax.axis_index("eig")

        def finish(piece):
            weights = piece[:samples].astype(jnp.bfloat16)
            sums = piece[samples:]
            high = sums.astype(jnp.bfloat16)
            low = (sums - high.astype(jnp.float32)).astype(jnp.bfloat16)
            return jnp.concatenate([weights, high, low], 0)

        def operate(vector):
            lowered = vector.astype(jnp.bfloat16)
            coeff = jnp.dot(
                lax.all_gather(lowered, "eig", axis=0, tiled=True),
                features,
                preferred_element_type=jnp.float32,
            )
            sums = jnp.zeros((8, group), jnp.float32)
            sums = sums.at[0, :own].set(jnp.sum(vector * vector, axis=1))
            sums = sums.at[1, :own].set(jnp.sum(noise_var[None, :] * vector * vector, axis=1))
            gathered = butterfly(
                jnp.concatenate([coeff * spectrum[None, :], sums], 0), n_vert, finish
            )
            weights = gathered[:samples]
            sums = gathered[samples : samples + 8].astype(jnp.float32) + gathered[
                samples + 8 : samples + 16
            ].astype(jnp.float32)
            wide = weights.astype(jnp.float32)
            energy = jnp.sum(wide * wide / spectrum[None, :], axis=1)
            if n_eig == 2:
                mine = lax.dynamic_slice_in_dim(energy, me_eig * own, own)
                theirs = lax.dynamic_slice_in_dim(energy, (1 - me_eig) * own, own)
                energy = mine + lax.ppermute(theirs, "eig", [(0, 1), (1, 0)])
            else:
                energy = lax.psum_scatter(energy, "eig", scatter_dimension=0, tiled=True)
            applied = lax.psum_scatter(
                lax.dot_general(
                    weights, features, (((1,), (1,)), ((), ())), preferred_element_type=jnp.float32
                ).astype(jnp.bfloat16),
                "eig",
                scatter_dimension=0,
                tiled=True,
            ).astype(jnp.float32)
            norm = sums[0, :own]
            product = sums[1, :own] + energy
            return applied + noise_var[None, :] * vector, norm, product

        residual = jnp.where(filled[None, :], rhs, jnp.zeros((), jnp.float32))
        solution = jnp.zeros_like(residual)
        applied, norm_now, product = operate(residual)
        step_size = norm_now / product
        direction, along = (residual, applied)
        for iteration in range(ITERS):
            solution = solution + step_size[:, None] * direction
            residual = residual - step_size[:, None] * along
            if iteration + 1 < ITERS:
                applied, norm_next, product = operate(residual)
                beta_ratio = norm_next / norm_now
                step_size = norm_next / (product - beta_ratio * norm_next / step_size)
                direction = residual + beta_ratio[:, None] * direction
                along = applied + beta_ratio[:, None] * along
                norm_now = norm_next
        return (solution, residual)

    return shards


def solution(mesh):
    return jax.shard_map(
        make_shards(mesh.shape["vert"], mesh.shape["eig"]),
        mesh=mesh,
        in_specs=(P("vert", "eig"), P("vert"), P("vert"), P("vert"), P("eig"), P("eig", "vert")),
        out_specs=(P("eig", "vert"), P("eig", "vert")),
        check_vma=False,
    )
```

```python
import jax
import jax.numpy as jnp
from jax import lax
from jax.sharding import PartitionSpec as P

ITERS = 2


def vert_sum(x, n_vert, finish):
    bits = n_vert.bit_length() - 1
    rounds = [list(range(b, min(b + 2, bits))) for b in range(0, bits, 2)]
    me = lax.axis_index("vert")
    cur = x
    plan = []
    for group in rounds:
        n = 1 << len(group)
        digit = sum(((me >> b) & 1) << i for i, b in enumerate(group))
        masks = [sum(((t >> i) & 1) << b for i, b in enumerate(group)) for t in range(n)]
        width = cur.shape[1] // n
        total = lax.dynamic_slice_in_dim(cur, digit * width, width, axis=1)
        for t in range(1, n):
            send = lax.dynamic_slice_in_dim(cur, (digit ^ t) * width, width, axis=1)
            total = total + lax.ppermute(send, "vert", [(i, i ^ masks[t]) for i in range(n_vert)])
        cur = total
        plan.append((n, digit, masks))
    cur = finish(cur)
    for n, digit, masks in reversed(plan):
        width = cur.shape[1]
        out = jnp.zeros((cur.shape[0], width * n), cur.dtype)
        out = lax.dynamic_update_slice_in_dim(out, cur, digit * width, axis=1)
        for t in range(1, n):
            got = lax.ppermute(cur, "vert", [(i, i ^ masks[t]) for i in range(n_vert)])
            out = lax.dynamic_update_slice_in_dim(out, got, (digit ^ t) * width, axis=1)
        cur = out
    return cur


def make_shards(n_vert, n_eig):
    pair = n_eig == 2
    swap = [(0, 1), (1, 0)]

    def shards(eig_table, obs_ids, counts, noise_var, eigenvalues, rhs):
        capacity = obs_ids.shape[0]
        own = rhs.shape[0]
        samples = own * n_eig
        group = eig_table.shape[1]
        filled = jnp.arange(capacity, dtype=jnp.int32) < counts[0]
        features = jnp.take(eig_table, obs_ids, axis=0)
        spectrum = 5.0 * jnp.power(3.0 + eigenvalues, -1.5)
        me_eig = lax.axis_index("eig")

        def finish(piece):
            weights = piece[:samples].astype(jnp.bfloat16)
            sums = piece[samples:]
            high = sums.astype(jnp.bfloat16)
            low = (sums - high.astype(jnp.float32)).astype(jnp.bfloat16)
            return jnp.concatenate([weights, high, low], 0)

        def operate(vector):
            lowered = vector.astype(jnp.bfloat16)
            if pair:
                rows = jnp.concatenate([lowered, lax.ppermute(lowered, "eig", swap)], 0)
            else:
                rows = lax.all_gather(lowered, "eig", axis=0, tiled=True)
            coeff = jnp.dot(rows, features, preferred_element_type=jnp.float32)
            sums = jnp.zeros((8, group), jnp.float32)
            sums = sums.at[0, :own].set(jnp.sum(vector * vector, axis=1))
            sums = sums.at[1, :own].set(jnp.sum(noise_var[None, :] * vector * vector, axis=1))
            gathered = vert_sum(
                jnp.concatenate([coeff * spectrum[None, :], sums], 0), n_vert, finish
            )
            weights = gathered[:samples]
            sums = gathered[samples : samples + 8].astype(jnp.float32) + gathered[
                samples + 8 : samples + 16
            ].astype(jnp.float32)
            wide = weights.astype(jnp.float32)
            energy = jnp.sum(wide * wide / spectrum[None, :], axis=1)
            partials = lax.dot_general(
                weights, features, (((1,), (1,)), ((), ())), preferred_element_type=jnp.float32
            ).astype(jnp.bfloat16)
            if pair:
                energy = energy[:own] + lax.ppermute(energy[own:], "eig", swap)
                image = partials[:own].astype(jnp.float32) + lax.ppermute(
                    partials[own:], "eig", swap
                ).astype(jnp.float32)
            else:
                energy = lax.psum_scatter(energy, "eig", scatter_dimension=0, tiled=True)
                image = lax.psum_scatter(
                    partials, "eig", scatter_dimension=0, tiled=True
                ).astype(jnp.float32)
            image = jnp.where(filled[None, :], image, jnp.zeros((), jnp.float32))
            norm = sums[0, :own]
            product = sums[1, :own] + energy
            return image + noise_var[None, :] * vector, norm, product

        residual = jnp.where(filled[None, :], rhs, jnp.zeros((), jnp.float32))
        solution = jnp.zeros_like(residual)
        applied, norm_now, product = operate(residual)
        step_size = norm_now / product
        direction, along = (residual, applied)
        for iteration in range(ITERS):
            solution = solution + step_size[:, None] * direction
            residual = residual - step_size[:, None] * along
            if iteration + 1 < ITERS:
                applied, norm_next, product = operate(residual)
                beta_ratio = norm_next / norm_now
                step_size = norm_next / (product - beta_ratio * norm_next / step_size)
                direction = residual + beta_ratio[:, None] * direction
                along = applied + beta_ratio[:, None] * along
                norm_now = norm_next
        return (solution, residual)

    return shards


def solution(mesh):
    return jax.shard_map(
        make_shards(mesh.shape["vert"], mesh.shape["eig"]),
        mesh=mesh,
        in_specs=(P("vert", "eig"), P("vert"), P("vert"), P("vert"), P("eig"), P("eig", "vert")),
        out_specs=(P("eig", "vert"), P("eig", "vert")),
        check_vma=False,
    )
```

```python
import jax
import jax.numpy as jnp
from jax import lax
from jax.sharding import PartitionSpec as P

ITERS = 2


def vert_sum(x, n_vert, finish, encode, decode):
    bits = n_vert.bit_length() - 1
    rounds = [list(range(b, min(b + 2, bits))) for b in range(0, bits, 2)]
    me = lax.axis_index("vert")
    cur = x
    plan = []
    for first, group in enumerate(rounds):
        n = 1 << len(group)
        digit = sum(((me >> b) & 1) << i for i, b in enumerate(group))
        masks = [sum(((t >> i) & 1) << b for i, b in enumerate(group)) for t in range(n)]
        width = cur.shape[1] // n
        total = lax.dynamic_slice_in_dim(cur, digit * width, width, axis=1)
        for t in range(1, n):
            send = lax.dynamic_slice_in_dim(cur, (digit ^ t) * width, width, axis=1)
            if first == 0:
                send = encode(send)
            got = lax.ppermute(send, "vert", [(i, i ^ masks[t]) for i in range(n_vert)])
            total = total + (decode(got) if first == 0 else got)
        cur = total
        plan.append((n, digit, masks))
    cur = finish(cur)
    for n, digit, masks in reversed(plan):
        width = cur.shape[1]
        out = jnp.zeros((cur.shape[0], width * n), cur.dtype)
        out = lax.dynamic_update_slice_in_dim(out, cur, digit * width, axis=1)
        for t in range(1, n):
            got = lax.ppermute(cur, "vert", [(i, i ^ masks[t]) for i in range(n_vert)])
            out = lax.dynamic_update_slice_in_dim(out, got, (digit ^ t) * width, axis=1)
        cur = out
    return cur


def make_shards(n_vert, n_eig):
    pair = n_eig == 2
    swap = [(0, 1), (1, 0)]

    def shards(eig_table, obs_ids, counts, noise_var, eigenvalues, rhs):
        capacity = obs_ids.shape[0]
        own = rhs.shape[0]
        samples = own * n_eig
        group = eig_table.shape[1]
        filled = jnp.arange(capacity, dtype=jnp.int32) < counts[0]
        features = jnp.take(eig_table, obs_ids, axis=0)
        spectrum = 5.0 * jnp.power(3.0 + eigenvalues, -1.5)
        me_eig = lax.axis_index("eig")

        def finish(piece):
            weights = piece[:samples].astype(jnp.bfloat16)
            sums = piece[samples:]
            high = sums.astype(jnp.bfloat16)
            low = (sums - high.astype(jnp.float32)).astype(jnp.bfloat16)
            return jnp.concatenate([weights, high, low], 0)

        def decode(block):
            return jnp.concatenate(
                [
                    block[:samples].astype(jnp.float32),
                    block[samples : samples + 8].astype(jnp.float32)
                    + block[samples + 8 :].astype(jnp.float32),
                ],
                0,
            )

        def operate(vector):
            lowered = vector.astype(jnp.bfloat16)
            if pair:
                rows = jnp.concatenate([lowered, lax.ppermute(lowered, "eig", swap)], 0)
            else:
                rows = lax.all_gather(lowered, "eig", axis=0, tiled=True)
            coeff = jnp.dot(rows, features, preferred_element_type=jnp.float32)
            sums = jnp.zeros((8, group), jnp.float32)
            sums = sums.at[0, :own].set(jnp.sum(vector * vector, axis=1))
            sums = sums.at[1, :own].set(jnp.sum(noise_var[None, :] * vector * vector, axis=1))
            gathered = vert_sum(
                jnp.concatenate([coeff * spectrum[None, :], sums], 0), n_vert, finish, finish, decode
            )
            weights = gathered[:samples]
            sums = gathered[samples : samples + 8].astype(jnp.float32) + gathered[
                samples + 8 : samples + 16
            ].astype(jnp.float32)
            wide = weights.astype(jnp.float32)
            energy = jnp.sum(wide * wide / spectrum[None, :], axis=1)
            partials = lax.dot_general(
                weights, features, (((1,), (1,)), ((), ())), preferred_element_type=jnp.float32
            ).astype(jnp.bfloat16)
            if pair:
                energy = energy[:own] + lax.ppermute(energy[own:], "eig", swap)
                image = partials[:own].astype(jnp.float32) + lax.ppermute(
                    partials[own:], "eig", swap
                ).astype(jnp.float32)
            else:
                energy = lax.psum_scatter(energy, "eig", scatter_dimension=0, tiled=True)
                image = lax.psum_scatter(
                    partials, "eig", scatter_dimension=0, tiled=True
                ).astype(jnp.float32)
            image = jnp.where(filled[None, :], image, jnp.zeros((), jnp.float32))
            norm = sums[0, :own]
            product = sums[1, :own] + energy
            return image + noise_var[None, :] * vector, norm, product

        residual = jnp.where(filled[None, :], rhs, jnp.zeros((), jnp.float32))
        solution = jnp.zeros_like(residual)
        applied, norm_now, product = operate(residual)
        step_size = norm_now / product
        direction, along = (residual, applied)
        for iteration in range(ITERS):
            solution = solution + step_size[:, None] * direction
            residual = residual - step_size[:, None] * along
            if iteration + 1 < ITERS:
                applied, norm_next, product = operate(residual)
                beta_ratio = norm_next / norm_now
                step_size = norm_next / (product - beta_ratio * norm_next / step_size)
                direction = residual + beta_ratio[:, None] * direction
                along = applied + beta_ratio[:, None] * along
                norm_now = norm_next
        return (solution, residual)

    return shards


def solution(mesh):
    return jax.shard_map(
        make_shards(mesh.shape["vert"], mesh.shape["eig"]),
        mesh=mesh,
        in_specs=(P("vert", "eig"), P("vert"), P("vert"), P("vert"), P("eig"), P("eig", "vert")),
        out_specs=(P("eig", "vert"), P("eig", "vert")),
        check_vma=False,
    )
```

```python
import jax
import jax.numpy as jnp
from jax import lax
from jax.sharding import PartitionSpec as P

ITERS = 2
CHUNKS = 2


def vert_sum(x, n_vert, finish, encode, decode):
    bits = n_vert.bit_length() - 1
    rounds = [list(range(b, min(b + 2, bits))) for b in range(0, bits, 2)]
    me = lax.axis_index("vert")
    cur = x
    plan = []
    for first, group in enumerate(rounds):
        n = 1 << len(group)
        digit = sum(((me >> b) & 1) << i for i, b in enumerate(group))
        masks = [sum(((t >> i) & 1) << b for i, b in enumerate(group)) for t in range(n)]
        width = cur.shape[1] // n
        total = lax.dynamic_slice_in_dim(cur, digit * width, width, axis=1)
        for t in range(1, n):
            send = lax.dynamic_slice_in_dim(cur, (digit ^ t) * width, width, axis=1)
            if first == 0:
                send = encode(send)
            got = lax.ppermute(send, "vert", [(i, i ^ masks[t]) for i in range(n_vert)])
            total = total + (decode(got) if first == 0 else got)
        cur = total
        plan.append((n, digit, masks))
    cur = finish(cur)
    for n, digit, masks in reversed(plan):
        width = cur.shape[1]
        out = jnp.zeros((cur.shape[0], width * n), cur.dtype)
        out = lax.dynamic_update_slice_in_dim(out, cur, digit * width, axis=1)
        for t in range(1, n):
            got = lax.ppermute(cur, "vert", [(i, i ^ masks[t]) for i in range(n_vert)])
            out = lax.dynamic_update_slice_in_dim(out, got, (digit ^ t) * width, axis=1)
        cur = out
    return cur


def make_shards(n_vert, n_eig):
    pair = n_eig == 2
    swap = [(0, 1), (1, 0)]

    def shards(eig_table, obs_ids, counts, noise_var, eigenvalues, rhs):
        capacity = obs_ids.shape[0]
        own = rhs.shape[0]
        samples = own * n_eig
        group = eig_table.shape[1]
        filled = jnp.arange(capacity, dtype=jnp.int32) < counts[0]
        width = group // CHUNKS
        def gather(table, c):
            return jnp.take(table[:, c * width : (c + 1) * width], obs_ids, axis=0)

        features = [gather(eig_table, c) for c in range(CHUNKS)]
        spectrum_all = 5.0 * jnp.power(3.0 + eigenvalues, -1.5)
        spectra = [spectrum_all[c * width : (c + 1) * width] for c in range(CHUNKS)]
        me_eig = lax.axis_index("eig")

        def finish(piece):
            weights = piece[:samples].astype(jnp.bfloat16)
            sums = piece[samples:]
            high = sums.astype(jnp.bfloat16)
            low = (sums - high.astype(jnp.float32)).astype(jnp.bfloat16)
            return jnp.concatenate([weights, high, low], 0)

        def decode(block):
            return jnp.concatenate(
                [
                    block[:samples].astype(jnp.float32),
                    block[samples : samples + 8].astype(jnp.float32)
                    + block[samples + 8 :].astype(jnp.float32),
                ],
                0,
            )

        def operate(vector):
            lowered = vector.astype(jnp.bfloat16)
            if pair:
                rows = jnp.concatenate([lowered, lax.ppermute(lowered, "eig", swap)], 0)
            else:
                rows = lax.all_gather(lowered, "eig", axis=0, tiled=True)
            sums = jnp.zeros((8, width), jnp.float32)
            sums = sums.at[0, :own].set(jnp.sum(vector * vector, axis=1))
            sums = sums.at[1, :own].set(jnp.sum(noise_var[None, :] * vector * vector, axis=1))
            energy = 0.0
            accumulated = None
            for c in range(CHUNKS):
                coeff = jnp.dot(rows, features[c], preferred_element_type=jnp.float32)
                block = jnp.concatenate(
                    [coeff * spectra[c][None, :], sums if c == 0 else jnp.zeros_like(sums)], 0
                )
                gathered = vert_sum(block, n_vert, finish, finish, decode)
                weights = gathered[:samples]
                if c == 0:
                    totals = gathered[samples : samples + 8].astype(jnp.float32) + gathered[
                        samples + 8 : samples + 16
                    ].astype(jnp.float32)
                wide = weights.astype(jnp.float32)
                energy = energy + jnp.sum(wide * wide / spectra[c][None, :], axis=1)
                term = lax.dot_general(
                    weights, features[c], (((1,), (1,)), ((), ())), preferred_element_type=jnp.float32
                )
                accumulated = term if accumulated is None else accumulated + term
            sums = totals
            partials = accumulated.astype(jnp.bfloat16)
            if pair:
                energy = energy[:own] + lax.ppermute(energy[own:], "eig", swap)
                image = partials[:own].astype(jnp.float32) + lax.ppermute(
                    partials[own:], "eig", swap
                ).astype(jnp.float32)
            else:
                energy = lax.psum_scatter(energy, "eig", scatter_dimension=0, tiled=True)
                image = lax.psum_scatter(
                    partials, "eig", scatter_dimension=0, tiled=True
                ).astype(jnp.float32)
            image = jnp.where(filled[None, :], image, jnp.zeros((), jnp.float32))
            norm = sums[0, :own]
            product = sums[1, :own] + energy
            return image + noise_var[None, :] * vector, norm, product

        residual = jnp.where(filled[None, :], rhs, jnp.zeros((), jnp.float32))
        solution = jnp.zeros_like(residual)
        applied, norm_now, product = operate(residual)
        step_size = norm_now / product
        direction, along = (residual, applied)
        for iteration in range(ITERS):
            solution = solution + step_size[:, None] * direction
            residual = residual - step_size[:, None] * along
            if iteration + 1 < ITERS:
                applied, norm_next, product = operate(residual)
                beta_ratio = norm_next / norm_now
                step_size = norm_next / (product - beta_ratio * norm_next / step_size)
                direction = residual + beta_ratio[:, None] * direction
                along = applied + beta_ratio[:, None] * along
                norm_now = norm_next
        return (solution, residual)

    return shards


def solution(mesh):
    return jax.shard_map(
        make_shards(mesh.shape["vert"], mesh.shape["eig"]),
        mesh=mesh,
        in_specs=(P("vert", "eig"), P("vert"), P("vert"), P("vert"), P("eig"), P("eig", "vert")),
        out_specs=(P("eig", "vert"), P("eig", "vert")),
        check_vma=False,
    )
```

```python
import jax
import jax.numpy as jnp
from jax import lax
from jax.sharding import PartitionSpec as P

ITERS = 2


def vert_sum(x, n_vert, finish, encode, decode):
    bits = n_vert.bit_length() - 1
    rounds = [list(range(b, min(b + 2, bits))) for b in range(0, bits, 2)]
    me = lax.axis_index("vert")
    cur = x
    plan = []
    for group in rounds:
        n = 1 << len(group)
        digit = sum(((me >> b) & 1) << i for i, b in enumerate(group))
        masks = [sum(((t >> i) & 1) << b for i, b in enumerate(group)) for t in range(n)]
        width = cur.shape[1] // n
        total = lax.dynamic_slice_in_dim(cur, digit * width, width, axis=1)
        for t in range(1, n):
            send = lax.dynamic_slice_in_dim(cur, (digit ^ t) * width, width, axis=1)
            got = lax.ppermute(encode(send), "vert", [(i, i ^ masks[t]) for i in range(n_vert)])
            total = total + decode(got)
        cur = total
        plan.append((n, digit, masks))
    cur = finish(cur)
    for n, digit, masks in reversed(plan):
        width = cur.shape[1]
        out = jnp.zeros((cur.shape[0], width * n), cur.dtype)
        out = lax.dynamic_update_slice_in_dim(out, cur, digit * width, axis=1)
        for t in range(1, n):
            got = lax.ppermute(cur, "vert", [(i, i ^ masks[t]) for i in range(n_vert)])
            out = lax.dynamic_update_slice_in_dim(out, got, (digit ^ t) * width, axis=1)
        cur = out
    return cur


def make_shards(n_vert, n_eig):
    pair = n_eig == 2
    swap = [(0, 1), (1, 0)]

    def shards(eig_table, obs_ids, counts, noise_var, eigenvalues, rhs):
        capacity = obs_ids.shape[0]
        own = rhs.shape[0]
        samples = own * n_eig
        group = eig_table.shape[1]
        filled = jnp.arange(capacity, dtype=jnp.int32) < counts[0]
        features = jnp.take(eig_table, obs_ids, axis=0)
        spectrum = 5.0 * jnp.power(3.0 + eigenvalues, -1.5)
        me_eig = lax.axis_index("eig")

        def finish(piece):
            weights = piece[:samples].astype(jnp.bfloat16)
            sums = piece[samples:]
            high = sums.astype(jnp.bfloat16)
            low = (sums - high.astype(jnp.float32)).astype(jnp.bfloat16)
            return jnp.concatenate([weights, high, low], 0)

        def decode(block):
            return jnp.concatenate(
                [
                    block[:samples].astype(jnp.float32),
                    block[samples : samples + 8].astype(jnp.float32)
                    + block[samples + 8 :].astype(jnp.float32),
                ],
                0,
            )

        def operate(vector):
            lowered = vector.astype(jnp.bfloat16)
            if pair:
                rows = jnp.concatenate([lowered, lax.ppermute(lowered, "eig", swap)], 0)
            else:
                rows = lax.all_gather(lowered, "eig", axis=0, tiled=True)
            coeff = jnp.dot(rows, features, preferred_element_type=jnp.float32)
            sums = jnp.zeros((8, group), jnp.float32)
            sums = sums.at[0, :own].set(jnp.sum(vector * vector, axis=1))
            sums = sums.at[1, :own].set(jnp.sum(noise_var[None, :] * vector * vector, axis=1))
            gathered = vert_sum(
                jnp.concatenate([coeff * spectrum[None, :], sums], 0), n_vert, finish, finish, decode
            )
            weights = gathered[:samples]
            sums = gathered[samples : samples + 8].astype(jnp.float32) + gathered[
                samples + 8 : samples + 16
            ].astype(jnp.float32)
            wide = weights.astype(jnp.float32)
            energy = jnp.sum(wide * wide / spectrum[None, :], axis=1)
            partials = lax.dot_general(
                weights, features, (((1,), (1,)), ((), ())), preferred_element_type=jnp.float32
            ).astype(jnp.bfloat16)
            if pair:
                energy = energy[:own] + lax.ppermute(energy[own:], "eig", swap)
                image = partials[:own].astype(jnp.float32) + lax.ppermute(
                    partials[own:], "eig", swap
                ).astype(jnp.float32)
            else:
                energy = lax.psum_scatter(energy, "eig", scatter_dimension=0, tiled=True)
                image = lax.psum_scatter(
                    partials, "eig", scatter_dimension=0, tiled=True
                ).astype(jnp.float32)
            image = jnp.where(filled[None, :], image, jnp.zeros((), jnp.float32))
            norm = sums[0, :own]
            product = sums[1, :own] + energy
            return image + noise_var[None, :] * vector, norm, product

        residual = jnp.where(filled[None, :], rhs, jnp.zeros((), jnp.float32))
        solution = jnp.zeros_like(residual)
        applied, norm_now, product = operate(residual)
        step_size = norm_now / product
        direction, along = (residual, applied)
        for iteration in range(ITERS):
            solution = solution + step_size[:, None] * direction
            residual = residual - step_size[:, None] * along
            if iteration + 1 < ITERS:
                applied, norm_next, product = operate(residual)
                beta_ratio = norm_next / norm_now
                step_size = norm_next / (product - beta_ratio * norm_next / step_size)
                direction = residual + beta_ratio[:, None] * direction
                along = applied + beta_ratio[:, None] * along
                norm_now = norm_next
        return (solution, residual)

    return shards


def solution(mesh):
    return jax.shard_map(
        make_shards(mesh.shape["vert"], mesh.shape["eig"]),
        mesh=mesh,
        in_specs=(P("vert", "eig"), P("vert"), P("vert"), P("vert"), P("eig"), P("eig", "vert")),
        out_specs=(P("eig", "vert"), P("eig", "vert")),
        check_vma=False,
    )
```

```python
import jax
import jax.numpy as jnp
from jax import lax
from jax.sharding import PartitionSpec as P

ITERS = 2


def vert_sum(x, n_vert, finish, encode, decode):
    bits = n_vert.bit_length() - 1
    rounds = [list(range(b, min(b + 2, bits))) for b in range(0, bits, 2)]
    me = lax.axis_index("vert")
    cur = x
    plan = []
    for group in rounds:
        n = 1 << len(group)
        digit = sum(((me >> b) & 1) << i for i, b in enumerate(group))
        masks = [sum(((t >> i) & 1) << b for i, b in enumerate(group)) for t in range(n)]
        width = cur.shape[1] // n
        total = lax.dynamic_slice_in_dim(cur, digit * width, width, axis=1)
        for t in range(1, n):
            send = lax.dynamic_slice_in_dim(cur, (digit ^ t) * width, width, axis=1)
            got = lax.ppermute(encode(send), "vert", [(i, i ^ masks[t]) for i in range(n_vert)])
            total = total + decode(got)
        cur = total
        plan.append((n, digit, masks))
    cur = finish(cur)
    for n, digit, masks in reversed(plan):
        width = cur.shape[1]
        out = jnp.zeros((cur.shape[0], width * n), cur.dtype)
        out = lax.dynamic_update_slice_in_dim(out, cur, digit * width, axis=1)
        for t in range(1, n):
            got = lax.ppermute(cur, "vert", [(i, i ^ masks[t]) for i in range(n_vert)])
            out = lax.dynamic_update_slice_in_dim(out, got, (digit ^ t) * width, axis=1)
        cur = out
    return cur


def make_shards(n_vert, n_eig):
    pair = n_eig == 2
    swap = [(0, 1), (1, 0)]

    def shards(eig_table, obs_ids, counts, noise_var, eigenvalues, rhs):
        capacity = obs_ids.shape[0]
        own = rhs.shape[0]
        samples = own * n_eig
        group = eig_table.shape[1]
        filled = jnp.arange(capacity, dtype=jnp.int32) < counts[0]
        picker = (obs_ids[:, None] == jnp.arange(eig_table.shape[0], dtype=jnp.int32)[None, :]).astype(
            jnp.bfloat16
        )
        features = jnp.dot(picker, eig_table, preferred_element_type=jnp.float32).astype(jnp.bfloat16)
        spectrum = 5.0 * jnp.power(3.0 + eigenvalues, -1.5)
        me_eig = lax.axis_index("eig")

        def finish(piece):
            weights = piece[:samples].astype(jnp.bfloat16)
            sums = piece[samples:]
            high = sums.astype(jnp.bfloat16)
            low = (sums - high.astype(jnp.float32)).astype(jnp.bfloat16)
            return jnp.concatenate([weights, high, low], 0)

        def decode(block):
            return jnp.concatenate(
                [
                    block[:samples].astype(jnp.float32),
                    block[samples : samples + 8].astype(jnp.float32)
                    + block[samples + 8 :].astype(jnp.float32),
                ],
                0,
            )

        def operate(vector):
            lowered = vector.astype(jnp.bfloat16)
            if pair:
                rows = jnp.concatenate([lowered, lax.ppermute(lowered, "eig", swap)], 0)
            else:
                rows = lax.all_gather(lowered, "eig", axis=0, tiled=True)
            coeff = jnp.dot(rows, features, preferred_element_type=jnp.float32)
            sums = jnp.zeros((8, group), jnp.float32)
            sums = sums.at[0, :own].set(jnp.sum(vector * vector, axis=1))
            sums = sums.at[1, :own].set(jnp.sum(noise_var[None, :] * vector * vector, axis=1))
            gathered = vert_sum(
                jnp.concatenate([coeff * spectrum[None, :], sums], 0), n_vert, finish, finish, decode
            )
            weights = gathered[:samples]
            sums = gathered[samples : samples + 8].astype(jnp.float32) + gathered[
                samples + 8 : samples + 16
            ].astype(jnp.float32)
            wide = weights.astype(jnp.float32)
            energy = jnp.sum(wide * wide / spectrum[None, :], axis=1)
            partials = lax.dot_general(
                weights, features, (((1,), (1,)), ((), ())), preferred_element_type=jnp.float32
            ).astype(jnp.bfloat16)
            if pair:
                energy = energy[:own] + lax.ppermute(energy[own:], "eig", swap)
                image = partials[:own].astype(jnp.float32) + lax.ppermute(
                    partials[own:], "eig", swap
                ).astype(jnp.float32)
            else:
                energy = lax.psum_scatter(energy, "eig", scatter_dimension=0, tiled=True)
                image = lax.psum_scatter(
                    partials, "eig", scatter_dimension=0, tiled=True
                ).astype(jnp.float32)
            image = jnp.where(filled[None, :], image, jnp.zeros((), jnp.float32))
            norm = sums[0, :own]
            product = sums[1, :own] + energy
            return image + noise_var[None, :] * vector, norm, product

        residual = jnp.where(filled[None, :], rhs, jnp.zeros((), jnp.float32))
        solution = jnp.zeros_like(residual)
        applied, norm_now, product = operate(residual)
        step_size = norm_now / product
        direction, along = (residual, applied)
        for iteration in range(ITERS):
            solution = solution + step_size[:, None] * direction
            residual = residual - step_size[:, None] * along
            if iteration + 1 < ITERS:
                applied, norm_next, product = operate(residual)
                beta_ratio = norm_next / norm_now
                step_size = norm_next / (product - beta_ratio * norm_next / step_size)
                direction = residual + beta_ratio[:, None] * direction
                along = applied + beta_ratio[:, None] * along
                norm_now = norm_next
        return (solution, residual)

    return shards


def solution(mesh):
    return jax.shard_map(
        make_shards(mesh.shape["vert"], mesh.shape["eig"]),
        mesh=mesh,
        in_specs=(P("vert", "eig"), P("vert"), P("vert"), P("vert"), P("eig"), P("eig", "vert")),
        out_specs=(P("eig", "vert"), P("eig", "vert")),
        check_vma=False,
    )
```

```python
import jax
import jax.numpy as jnp
from jax import lax
from jax.sharding import PartitionSpec as P

ITERS = 2


def vert_sum(x, n_vert, finish, encode, decode):
    bits = n_vert.bit_length() - 1
    rounds = [list(range(b, min(b + 2, bits))) for b in range(0, bits, 2)]
    me = lax.axis_index("vert")
    cur = x
    plan = []
    for group in rounds:
        n = 1 << len(group)
        digit = sum(((me >> b) & 1) << i for i, b in enumerate(group))
        masks = [sum(((t >> i) & 1) << b for i, b in enumerate(group)) for t in range(n)]
        width = cur.shape[1] // n
        total = lax.dynamic_slice_in_dim(cur, digit * width, width, axis=1)
        for t in range(1, n):
            send = lax.dynamic_slice_in_dim(cur, (digit ^ t) * width, width, axis=1)
            got = lax.ppermute(encode(send), "vert", [(i, i ^ masks[t]) for i in range(n_vert)])
            total = total + decode(got)
        cur = total
        plan.append((n, digit, masks))
    cur = finish(cur)
    for n, digit, masks in reversed(plan):
        width = cur.shape[1]
        out = jnp.zeros((cur.shape[0], width * n), cur.dtype)
        out = lax.dynamic_update_slice_in_dim(out, cur, digit * width, axis=1)
        for t in range(1, n):
            got = lax.ppermute(cur, "vert", [(i, i ^ masks[t]) for i in range(n_vert)])
            out = lax.dynamic_update_slice_in_dim(out, got, (digit ^ t) * width, axis=1)
        cur = out
    return cur


def make_shards(n_vert, n_eig):
    pair = n_eig == 2
    swap = [(0, 1), (1, 0)]

    def shards(eig_table, obs_ids, counts, noise_var, eigenvalues, rhs):
        capacity = obs_ids.shape[0]
        own = rhs.shape[0]
        samples = own * n_eig
        group = eig_table.shape[1]
        filled = jnp.arange(capacity, dtype=jnp.int32) < counts[0]
        picker = (obs_ids[:, None] == jnp.arange(eig_table.shape[0], dtype=jnp.int32)[None, :]).astype(
            jnp.bfloat16
        )
        piece = group // 4
        features = jnp.concatenate(
            [
                jnp.dot(picker, eig_table[:, c * piece : (c + 1) * piece], preferred_element_type=jnp.float32)
                .astype(jnp.bfloat16)
                for c in range(4)
            ],
            1,
        )

        def coeff_from_table(rows):
            summed = jnp.dot(rows, picker, preferred_element_type=jnp.float32)
            high = summed.astype(jnp.bfloat16)
            low = (summed - high.astype(jnp.float32)).astype(jnp.bfloat16)
            both = jnp.dot(
                jnp.concatenate([high, low], 0), eig_table, preferred_element_type=jnp.float32
            )
            return both[: rows.shape[0]] + both[rows.shape[0] :]
        spectrum = 5.0 * jnp.power(3.0 + eigenvalues, -1.5)
        me_eig = lax.axis_index("eig")

        def finish(piece):
            weights = piece[:samples].astype(jnp.bfloat16)
            sums = piece[samples:]
            high = sums.astype(jnp.bfloat16)
            low = (sums - high.astype(jnp.float32)).astype(jnp.bfloat16)
            return jnp.concatenate([weights, high, low], 0)

        def decode(block):
            return jnp.concatenate(
                [
                    block[:samples].astype(jnp.float32),
                    block[samples : samples + 8].astype(jnp.float32)
                    + block[samples + 8 :].astype(jnp.float32),
                ],
                0,
            )

        def operate(vector, first=False):
            lowered = vector.astype(jnp.bfloat16)
            if pair:
                rows = jnp.concatenate([lowered, lax.ppermute(lowered, "eig", swap)], 0)
            else:
                rows = lax.all_gather(lowered, "eig", axis=0, tiled=True)
            if first:
                coeff = coeff_from_table(rows)
            else:
                coeff = jnp.dot(rows, features, preferred_element_type=jnp.float32)
            sums = jnp.zeros((8, group), jnp.float32)
            sums = sums.at[0, :own].set(jnp.sum(vector * vector, axis=1))
            sums = sums.at[1, :own].set(jnp.sum(noise_var[None, :] * vector * vector, axis=1))
            gathered = vert_sum(
                jnp.concatenate([coeff * spectrum[None, :], sums], 0), n_vert, finish, finish, decode
            )
            weights = gathered[:samples]
            sums = gathered[samples : samples + 8].astype(jnp.float32) + gathered[
                samples + 8 : samples + 16
            ].astype(jnp.float32)
            wide = weights.astype(jnp.float32)
            energy = jnp.sum(wide * wide / spectrum[None, :], axis=1)
            partials = lax.dot_general(
                weights, features, (((1,), (1,)), ((), ())), preferred_element_type=jnp.float32
            ).astype(jnp.bfloat16)
            if pair:
                energy = energy[:own] + lax.ppermute(energy[own:], "eig", swap)
                image = partials[:own].astype(jnp.float32) + lax.ppermute(
                    partials[own:], "eig", swap
                ).astype(jnp.float32)
            else:
                energy = lax.psum_scatter(energy, "eig", scatter_dimension=0, tiled=True)
                image = lax.psum_scatter(
                    partials, "eig", scatter_dimension=0, tiled=True
                ).astype(jnp.float32)
            image = jnp.where(filled[None, :], image, jnp.zeros((), jnp.float32))
            norm = sums[0, :own]
            product = sums[1, :own] + energy
            return image + noise_var[None, :] * vector, norm, product

        residual = jnp.where(filled[None, :], rhs, jnp.zeros((), jnp.float32))
        solution = jnp.zeros_like(residual)
        applied, norm_now, product = operate(residual, first=True)
        step_size = norm_now / product
        direction, along = (residual, applied)
        for iteration in range(ITERS):
            solution = solution + step_size[:, None] * direction
            residual = residual - step_size[:, None] * along
            if iteration + 1 < ITERS:
                applied, norm_next, product = operate(residual)
                beta_ratio = norm_next / norm_now
                step_size = norm_next / (product - beta_ratio * norm_next / step_size)
                direction = residual + beta_ratio[:, None] * direction
                along = applied + beta_ratio[:, None] * along
                norm_now = norm_next
        return (solution, residual)

    return shards


def solution(mesh):
    return jax.shard_map(
        make_shards(mesh.shape["vert"], mesh.shape["eig"]),
        mesh=mesh,
        in_specs=(P("vert", "eig"), P("vert"), P("vert"), P("vert"), P("eig"), P("eig", "vert")),
        out_specs=(P("eig", "vert"), P("eig", "vert")),
        check_vma=False,
    )
```

```python
import jax
import jax.numpy as jnp
from jax import lax
from jax.sharding import PartitionSpec as P

ITERS = 2


def vert_sum(x, n_vert, finish, encode, decode):
    bits = n_vert.bit_length() - 1
    rounds = [list(range(b, min(b + 2, bits))) for b in range(0, bits, 2)]
    me = lax.axis_index("vert")
    cur = x
    plan = []
    for group in rounds:
        n = 1 << len(group)
        digit = sum(((me >> b) & 1) << i for i, b in enumerate(group))
        masks = [sum(((t >> i) & 1) << b for i, b in enumerate(group)) for t in range(n)]
        width = cur.shape[1] // n
        total = lax.dynamic_slice_in_dim(cur, digit * width, width, axis=1)
        for t in range(1, n):
            send = lax.dynamic_slice_in_dim(cur, (digit ^ t) * width, width, axis=1)
            got = lax.ppermute(encode(send), "vert", [(i, i ^ masks[t]) for i in range(n_vert)])
            total = total + decode(got)
        cur = total
        plan.append((n, digit, masks))
    cur = finish(cur)
    for n, digit, masks in reversed(plan):
        width = cur.shape[1]
        out = jnp.zeros((cur.shape[0], width * n), cur.dtype)
        out = lax.dynamic_update_slice_in_dim(out, cur, digit * width, axis=1)
        for t in range(1, n):
            got = lax.ppermute(cur, "vert", [(i, i ^ masks[t]) for i in range(n_vert)])
            out = lax.dynamic_update_slice_in_dim(out, got, (digit ^ t) * width, axis=1)
        cur = out
    return cur


def make_shards(n_vert, n_eig):
    pair = n_eig == 2
    swap = [(0, 1), (1, 0)]

    def shards(eig_table, obs_ids, counts, noise_var, eigenvalues, rhs):
        capacity = obs_ids.shape[0]
        own = rhs.shape[0]
        samples = own * n_eig
        group = eig_table.shape[1]
        filled = jnp.arange(capacity, dtype=jnp.int32) < counts[0]
        picker = (obs_ids[:, None] == jnp.arange(eig_table.shape[0], dtype=jnp.int32)[None, :]).astype(
            jnp.bfloat16
        )
        features = jnp.dot(picker, eig_table, preferred_element_type=jnp.float32).astype(jnp.bfloat16)

        def coeff_from_table(rows):
            summed = jnp.dot(rows, picker, preferred_element_type=jnp.float32)
            high = summed.astype(jnp.bfloat16)
            low = (summed - high.astype(jnp.float32)).astype(jnp.bfloat16)
            both = jnp.dot(
                jnp.concatenate([high, low], 0), eig_table, preferred_element_type=jnp.float32
            )
            return both[: rows.shape[0]] + both[rows.shape[0] :]
        spectrum = 5.0 * jnp.power(3.0 + eigenvalues, -1.5)
        me_eig = lax.axis_index("eig")

        def finish(piece):
            weights = piece[:samples].astype(jnp.bfloat16)
            sums = piece[samples:]
            high = sums.astype(jnp.bfloat16)
            low = (sums - high.astype(jnp.float32)).astype(jnp.bfloat16)
            return jnp.concatenate([weights, high, low], 0)

        def decode(block):
            return jnp.concatenate(
                [
                    block[:samples].astype(jnp.float32),
                    block[samples : samples + 8].astype(jnp.float32)
                    + block[samples + 8 :].astype(jnp.float32),
                ],
                0,
            )

        def operate(vector, first=False):
            lowered = vector.astype(jnp.bfloat16)
            if pair:
                rows = jnp.concatenate([lowered, lax.ppermute(lowered, "eig", swap)], 0)
            else:
                rows = lax.all_gather(lowered, "eig", axis=0, tiled=True)
            if first:
                coeff = coeff_from_table(rows)
            else:
                coeff = jnp.dot(rows, features, preferred_element_type=jnp.float32)
            sums = jnp.zeros((8, group), jnp.float32)
            sums = sums.at[0, :own].set(jnp.sum(vector * vector, axis=1))
            sums = sums.at[1, :own].set(jnp.sum(noise_var[None, :] * vector * vector, axis=1))
            gathered = vert_sum(
                jnp.concatenate([coeff * spectrum[None, :], sums], 0), n_vert, finish, finish, decode
            )
            weights = gathered[:samples]
            sums = gathered[samples : samples + 8].astype(jnp.float32) + gathered[
                samples + 8 : samples + 16
            ].astype(jnp.float32)
            wide = weights.astype(jnp.float32)
            energy = jnp.sum(wide * wide / spectrum[None, :], axis=1)
            partials = lax.dot_general(
                weights, features, (((1,), (1,)), ((), ())), preferred_element_type=jnp.float32
            ).astype(jnp.bfloat16)
            if pair:
                energy = energy[:own] + lax.ppermute(energy[own:], "eig", swap)
                image = partials[:own].astype(jnp.float32) + lax.ppermute(
                    partials[own:], "eig", swap
                ).astype(jnp.float32)
            else:
                energy = lax.psum_scatter(energy, "eig", scatter_dimension=0, tiled=True)
                image = lax.psum_scatter(
                    partials, "eig", scatter_dimension=0, tiled=True
                ).astype(jnp.float32)
            image = jnp.where(filled[None, :], image, jnp.zeros((), jnp.float32))
            norm = sums[0, :own]
            product = sums[1, :own] + energy
            return image + noise_var[None, :] * vector, norm, product

        residual = jnp.where(filled[None, :], rhs, jnp.zeros((), jnp.float32))
        solution = jnp.zeros_like(residual)
        applied, norm_now, product = operate(residual, first=True)
        step_size = norm_now / product
        direction, along = (residual, applied)
        for iteration in range(ITERS):
            solution = solution + step_size[:, None] * direction
            residual = residual - step_size[:, None] * along
            if iteration + 1 < ITERS:
                applied, norm_next, product = operate(residual)
                beta_ratio = norm_next / norm_now
                step_size = norm_next / (product - beta_ratio * norm_next / step_size)
                direction = residual + beta_ratio[:, None] * direction
                along = applied + beta_ratio[:, None] * along
                norm_now = norm_next
        return (solution, residual)

    return shards


def solution(mesh):
    return jax.shard_map(
        make_shards(mesh.shape["vert"], mesh.shape["eig"]),
        mesh=mesh,
        in_specs=(P("vert", "eig"), P("vert"), P("vert"), P("vert"), P("eig"), P("eig", "vert")),
        out_specs=(P("eig", "vert"), P("eig", "vert")),
        check_vma=False,
    )
```

```python
import jax
import jax.numpy as jnp
from jax import lax
from jax.sharding import PartitionSpec as P

ITERS = 2


def vert_sum(x, n_vert, finish, encode, decode, side=()):
    side = list(side)

    def beside(k, sent, received):
        if k >= len(side):
            return received
        out = side[k](sent)
        received, out = lax.optimization_barrier((received, out))
        side[k] = out
        return received

    bits = n_vert.bit_length() - 1
    rounds = [list(range(b, min(b + 2, bits))) for b in range(0, bits, 2)]
    me = lax.axis_index("vert")
    cur = x
    plan = []
    for group in rounds:
        n = 1 << len(group)
        digit = sum(((me >> b) & 1) << i for i, b in enumerate(group))
        masks = [sum(((t >> i) & 1) << b for i, b in enumerate(group)) for t in range(n)]
        width = cur.shape[1] // n
        total = lax.dynamic_slice_in_dim(cur, digit * width, width, axis=1)
        sends = [
            encode(lax.dynamic_slice_in_dim(cur, (digit ^ t) * width, width, axis=1))
            for t in range(1, n)
        ]
        gots = [
            lax.ppermute(send, "vert", [(i, i ^ masks[t + 1]) for i in range(n_vert)])
            for t, send in enumerate(sends)
        ]
        gots = beside(len(plan), sends[0], gots)
        for got in gots:
            total = total + decode(got)
        cur = total
        plan.append((n, digit, masks))
    cur = finish(cur)
    for k, (n, digit, masks) in enumerate(reversed(plan), len(plan)):
        width = cur.shape[1]
        out = jnp.zeros((cur.shape[0], width * n), cur.dtype)
        out = lax.dynamic_update_slice_in_dim(out, cur, digit * width, axis=1)
        gots = [
            lax.ppermute(cur, "vert", [(i, i ^ masks[t]) for i in range(n_vert)]) for t in range(1, n)
        ]
        gots = beside(k, cur, gots)
        for t, got in enumerate(gots, 1):
            out = lax.dynamic_update_slice_in_dim(out, got, (digit ^ t) * width, axis=1)
        cur = out
    return cur, side


def make_shards(n_vert, n_eig):
    pair = n_eig == 2
    swap = [(0, 1), (1, 0)]

    def shards(eig_table, obs_ids, counts, noise_var, eigenvalues, rhs):
        capacity = obs_ids.shape[0]
        own = rhs.shape[0]
        samples = own * n_eig
        group = eig_table.shape[1]
        filled = jnp.arange(capacity, dtype=jnp.int32) < counts[0]
        vertices = jnp.arange(eig_table.shape[0], dtype=jnp.int32)
        picker = (obs_ids[:, None] == vertices[None, :]).astype(jnp.bfloat16)
        pieces = 4 if capacity % 32 == 0 else 1
        span = capacity // pieces

        def piece(p):
            def work(anchor):
                ids, _ = lax.optimization_barrier((obs_ids[p * span : (p + 1) * span], anchor))
                rows = (ids[:, None] == vertices[None, :]).astype(jnp.bfloat16)
                return jnp.dot(rows, eig_table, preferred_element_type=jnp.float32).astype(jnp.bfloat16)

            return work

        built = []

        def coeff_from_table(rows):
            summed = jnp.dot(rows, picker, preferred_element_type=jnp.float32)
            high = summed.astype(jnp.bfloat16)
            low = (summed - high.astype(jnp.float32)).astype(jnp.bfloat16)
            both = jnp.dot(
                jnp.concatenate([high, low], 0), eig_table, preferred_element_type=jnp.float32
            )
            return both[: rows.shape[0]] + both[rows.shape[0] :]
        spectrum = 5.0 * jnp.power(3.0 + eigenvalues, -1.5)
        me_eig = lax.axis_index("eig")

        def finish(piece):
            weights = piece[:samples].astype(jnp.bfloat16)
            sums = piece[samples:]
            high = sums.astype(jnp.bfloat16)
            low = (sums - high.astype(jnp.float32)).astype(jnp.bfloat16)
            return jnp.concatenate([weights, high, low], 0)

        def decode(block):
            return jnp.concatenate(
                [
                    block[:samples].astype(jnp.float32),
                    block[samples : samples + 8].astype(jnp.float32)
                    + block[samples + 8 :].astype(jnp.float32),
                ],
                0,
            )

        def operate(vector, first=False):
            lowered = vector.astype(jnp.bfloat16)
            if pair:
                rows = jnp.concatenate([lowered, lax.ppermute(lowered, "eig", swap)], 0)
            else:
                rows = lax.all_gather(lowered, "eig", axis=0, tiled=True)
            if first:
                coeff = coeff_from_table(rows)
            else:
                coeff = jnp.dot(rows, built[0], preferred_element_type=jnp.float32)
            sums = jnp.zeros((8, group), jnp.float32)
            sums = sums.at[0, :own].set(jnp.sum(vector * vector, axis=1))
            sums = sums.at[1, :own].set(jnp.sum(noise_var[None, :] * vector * vector, axis=1))
            gathered, side = vert_sum(
                jnp.concatenate([coeff * spectrum[None, :], sums], 0),
                n_vert,
                finish,
                finish,
                decode,
                [piece(p) for p in range(pieces)] if first else (),
            )
            if first:
                built.append(jnp.concatenate(side, 0))
            features = built[0]
            weights = gathered[:samples]
            sums = gathered[samples : samples + 8].astype(jnp.float32) + gathered[
                samples + 8 : samples + 16
            ].astype(jnp.float32)
            wide = weights.astype(jnp.float32)
            energy = jnp.sum(wide * wide / spectrum[None, :], axis=1)
            partials = lax.dot_general(
                weights, features, (((1,), (1,)), ((), ())), preferred_element_type=jnp.float32
            ).astype(jnp.bfloat16)
            if pair:
                energy = energy[:own] + lax.ppermute(energy[own:], "eig", swap)
                image = partials[:own].astype(jnp.float32) + lax.ppermute(
                    partials[own:], "eig", swap
                ).astype(jnp.float32)
            else:
                energy = lax.psum_scatter(energy, "eig", scatter_dimension=0, tiled=True)
                image = lax.psum_scatter(
                    partials, "eig", scatter_dimension=0, tiled=True
                ).astype(jnp.float32)
            image = jnp.where(filled[None, :], image, jnp.zeros((), jnp.float32))
            norm = sums[0, :own]
            product = sums[1, :own] + energy
            return image + noise_var[None, :] * vector, norm, product

        residual = jnp.where(filled[None, :], rhs, jnp.zeros((), jnp.float32))
        solution = jnp.zeros_like(residual)
        applied, norm_now, product = operate(residual, first=True)
        step_size = norm_now / product
        direction, along = (residual, applied)
        for iteration in range(ITERS):
            solution = solution + step_size[:, None] * direction
            residual = residual - step_size[:, None] * along
            if iteration + 1 < ITERS:
                applied, norm_next, product = operate(residual)
                beta_ratio = norm_next / norm_now
                step_size = norm_next / (product - beta_ratio * norm_next / step_size)
                direction = residual + beta_ratio[:, None] * direction
                along = applied + beta_ratio[:, None] * along
                norm_now = norm_next
        return (solution, residual)

    return shards


def solution(mesh):
    return jax.shard_map(
        make_shards(mesh.shape["vert"], mesh.shape["eig"]),
        mesh=mesh,
        in_specs=(P("vert", "eig"), P("vert"), P("vert"), P("vert"), P("eig"), P("eig", "vert")),
        out_specs=(P("eig", "vert"), P("eig", "vert")),
        check_vma=False,
    )
```

```python
import jax
import jax.numpy as jnp
from jax import lax
from jax.sharding import PartitionSpec as P

ITERS = 2
PIECES = 2


def vert_sum(x, n_vert, finish, encode, decode, side=()):
    side = list(side)

    def beside(k, sent, received):
        if k >= len(side):
            return received
        out = side[k](sent)
        received, out = lax.optimization_barrier((received, out))
        side[k] = out
        return received

    bits = n_vert.bit_length() - 1
    rounds = [list(range(b, min(b + 2, bits))) for b in range(0, bits, 2)]
    me = lax.axis_index("vert")
    cur = x
    plan = []
    for group in rounds:
        n = 1 << len(group)
        digit = sum(((me >> b) & 1) << i for i, b in enumerate(group))
        masks = [sum(((t >> i) & 1) << b for i, b in enumerate(group)) for t in range(n)]
        width = cur.shape[1] // n
        total = lax.dynamic_slice_in_dim(cur, digit * width, width, axis=1)
        sends = [
            encode(lax.dynamic_slice_in_dim(cur, (digit ^ t) * width, width, axis=1))
            for t in range(1, n)
        ]
        gots = [
            lax.ppermute(send, "vert", [(i, i ^ masks[t + 1]) for i in range(n_vert)])
            for t, send in enumerate(sends)
        ]
        gots = beside(len(plan), sends[0], gots)
        for got in gots:
            total = total + decode(got)
        cur = total
        plan.append((n, digit, masks))
    cur = finish(cur)
    for k, (n, digit, masks) in enumerate(reversed(plan), len(plan)):
        width = cur.shape[1]
        out = jnp.zeros((cur.shape[0], width * n), cur.dtype)
        out = lax.dynamic_update_slice_in_dim(out, cur, digit * width, axis=1)
        gots = [
            lax.ppermute(cur, "vert", [(i, i ^ masks[t]) for i in range(n_vert)]) for t in range(1, n)
        ]
        gots = beside(k, cur, gots)
        for t, got in enumerate(gots, 1):
            out = lax.dynamic_update_slice_in_dim(out, got, (digit ^ t) * width, axis=1)
        cur = out
    return cur, side


def make_shards(n_vert, n_eig):
    pair = n_eig == 2
    swap = [(0, 1), (1, 0)]

    def shards(eig_table, obs_ids, counts, noise_var, eigenvalues, rhs):
        capacity = obs_ids.shape[0]
        own = rhs.shape[0]
        samples = own * n_eig
        group = eig_table.shape[1]
        filled = jnp.arange(capacity, dtype=jnp.int32) < counts[0]
        vertices = jnp.arange(eig_table.shape[0], dtype=jnp.int32)
        picker = (obs_ids[:, None] == vertices[None, :]).astype(jnp.bfloat16)
        pieces = PIECES if capacity % (8 * PIECES) == 0 else 1
        span = capacity // pieces

        def piece(p):
            def work(anchor):
                ids, _ = lax.optimization_barrier((obs_ids[p * span : (p + 1) * span], anchor))
                rows = (ids[:, None] == vertices[None, :]).astype(jnp.bfloat16)
                return jnp.dot(rows, eig_table, preferred_element_type=jnp.float32).astype(jnp.bfloat16)

            return work

        built = []

        def coeff_from_table(rows):
            summed = jnp.dot(rows, picker, preferred_element_type=jnp.float32)
            high = summed.astype(jnp.bfloat16)
            low = (summed - high.astype(jnp.float32)).astype(jnp.bfloat16)
            both = jnp.dot(
                jnp.concatenate([high, low], 0), eig_table, preferred_element_type=jnp.float32
            )
            return both[: rows.shape[0]] + both[rows.shape[0] :]
        spectrum = 5.0 * jnp.power(3.0 + eigenvalues, -1.5)
        me_eig = lax.axis_index("eig")

        def finish(piece):
            weights = piece[:samples].astype(jnp.bfloat16)
            sums = piece[samples:]
            high = sums.astype(jnp.bfloat16)
            low = (sums - high.astype(jnp.float32)).astype(jnp.bfloat16)
            return jnp.concatenate([weights, high, low], 0)

        def decode(block):
            return jnp.concatenate(
                [
                    block[:samples].astype(jnp.float32),
                    block[samples : samples + 8].astype(jnp.float32)
                    + block[samples + 8 :].astype(jnp.float32),
                ],
                0,
            )

        def operate(vector, first=False):
            lowered = vector.astype(jnp.bfloat16)
            if pair:
                rows = jnp.concatenate([lowered, lax.ppermute(lowered, "eig", swap)], 0)
            else:
                rows = lax.all_gather(lowered, "eig", axis=0, tiled=True)
            if first:
                coeff = coeff_from_table(rows)
            else:
                coeff = jnp.dot(rows, built[0], preferred_element_type=jnp.float32)
            sums = jnp.zeros((8, group), jnp.float32)
            sums = sums.at[0, :own].set(jnp.sum(vector * vector, axis=1))
            sums = sums.at[1, :own].set(jnp.sum(noise_var[None, :] * vector * vector, axis=1))
            gathered, side = vert_sum(
                jnp.concatenate([coeff * spectrum[None, :], sums], 0),
                n_vert,
                finish,
                finish,
                decode,
                [piece(p) for p in range(pieces)] if first else (),
            )
            if first:
                built.append(jnp.concatenate(side, 0))
            features = built[0]
            weights = gathered[:samples]
            sums = gathered[samples : samples + 8].astype(jnp.float32) + gathered[
                samples + 8 : samples + 16
            ].astype(jnp.float32)
            wide = weights.astype(jnp.float32)
            energy = jnp.sum(wide * wide / spectrum[None, :], axis=1)
            partials = lax.dot_general(
                weights, features, (((1,), (1,)), ((), ())), preferred_element_type=jnp.float32
            ).astype(jnp.bfloat16)
            if pair:
                energy = energy[:own] + lax.ppermute(energy[own:], "eig", swap)
                image = partials[:own].astype(jnp.float32) + lax.ppermute(
                    partials[own:], "eig", swap
                ).astype(jnp.float32)
            else:
                energy = lax.psum_scatter(energy, "eig", scatter_dimension=0, tiled=True)
                image = lax.psum_scatter(
                    partials, "eig", scatter_dimension=0, tiled=True
                ).astype(jnp.float32)
            image = jnp.where(filled[None, :], image, jnp.zeros((), jnp.float32))
            norm = sums[0, :own]
            product = sums[1, :own] + energy
            return image + noise_var[None, :] * vector, norm, product

        residual = jnp.where(filled[None, :], rhs, jnp.zeros((), jnp.float32))
        solution = jnp.zeros_like(residual)
        applied, norm_now, product = operate(residual, first=True)
        step_size = norm_now / product
        direction, along = (residual, applied)
        for iteration in range(ITERS):
            solution = solution + step_size[:, None] * direction
            residual = residual - step_size[:, None] * along
            if iteration + 1 < ITERS:
                applied, norm_next, product = operate(residual)
                beta_ratio = norm_next / norm_now
                step_size = norm_next / (product - beta_ratio * norm_next / step_size)
                direction = residual + beta_ratio[:, None] * direction
                along = applied + beta_ratio[:, None] * along
                norm_now = norm_next
        return (solution, residual)

    return shards


def solution(mesh):
    return jax.shard_map(
        make_shards(mesh.shape["vert"], mesh.shape["eig"]),
        mesh=mesh,
        in_specs=(P("vert", "eig"), P("vert"), P("vert"), P("vert"), P("eig"), P("eig", "vert")),
        out_specs=(P("eig", "vert"), P("eig", "vert")),
        check_vma=False,
    )
```

```python
import jax
import jax.numpy as jnp
from jax import lax
from jax.sharding import PartitionSpec as P

ITERS = 2
PIECES = 3


def vert_sum(x, n_vert, finish, encode, decode, side=()):
    side = list(side)

    def beside(k, sent, received):
        if k >= len(side):
            return received
        out = side[k](sent)
        received, out = lax.optimization_barrier((received, out))
        side[k] = out
        return received

    bits = n_vert.bit_length() - 1
    rounds = [list(range(b, min(b + 2, bits))) for b in range(0, bits, 2)]
    me = lax.axis_index("vert")
    cur = x
    plan = []
    for group in rounds:
        n = 1 << len(group)
        digit = sum(((me >> b) & 1) << i for i, b in enumerate(group))
        masks = [sum(((t >> i) & 1) << b for i, b in enumerate(group)) for t in range(n)]
        width = cur.shape[1] // n
        total = lax.dynamic_slice_in_dim(cur, digit * width, width, axis=1)
        sends = [
            encode(lax.dynamic_slice_in_dim(cur, (digit ^ t) * width, width, axis=1))
            for t in range(1, n)
        ]
        gots = [
            lax.ppermute(send, "vert", [(i, i ^ masks[t + 1]) for i in range(n_vert)])
            for t, send in enumerate(sends)
        ]
        gots = beside(len(plan), sends[0], gots)
        for got in gots:
            total = total + decode(got)
        cur = total
        plan.append((n, digit, masks))
    cur = finish(cur)
    for k, (n, digit, masks) in enumerate(reversed(plan), len(plan)):
        width = cur.shape[1]
        out = jnp.zeros((cur.shape[0], width * n), cur.dtype)
        out = lax.dynamic_update_slice_in_dim(out, cur, digit * width, axis=1)
        gots = [
            lax.ppermute(cur, "vert", [(i, i ^ masks[t]) for i in range(n_vert)]) for t in range(1, n)
        ]
        gots = beside(k, cur, gots)
        for t, got in enumerate(gots, 1):
            out = lax.dynamic_update_slice_in_dim(out, got, (digit ^ t) * width, axis=1)
        cur = out
    return cur, side


def make_shards(n_vert, n_eig):
    pair = n_eig == 2
    swap = [(0, 1), (1, 0)]

    def shards(eig_table, obs_ids, counts, noise_var, eigenvalues, rhs):
        capacity = obs_ids.shape[0]
        own = rhs.shape[0]
        samples = own * n_eig
        group = eig_table.shape[1]
        filled = jnp.arange(capacity, dtype=jnp.int32) < counts[0]
        vertices = jnp.arange(eig_table.shape[0], dtype=jnp.int32)
        picker = (obs_ids[:, None] == vertices[None, :]).astype(jnp.bfloat16)
        pieces = PIECES if capacity % (8 * PIECES) == 0 else 1
        span = capacity // pieces

        def piece(p):
            def work(anchor):
                ids, _ = lax.optimization_barrier((obs_ids[p * span : (p + 1) * span], anchor))
                rows = (ids[:, None] == vertices[None, :]).astype(jnp.bfloat16)
                return jnp.dot(rows, eig_table, preferred_element_type=jnp.float32).astype(jnp.bfloat16)

            return work

        built = []

        def coeff_from_table(rows):
            summed = jnp.dot(rows, picker, preferred_element_type=jnp.float32)
            high = summed.astype(jnp.bfloat16)
            low = (summed - high.astype(jnp.float32)).astype(jnp.bfloat16)
            both = jnp.dot(
                jnp.concatenate([high, low], 0), eig_table, preferred_element_type=jnp.float32
            )
            return both[: rows.shape[0]] + both[rows.shape[0] :]
        spectrum = 5.0 * jnp.power(3.0 + eigenvalues, -1.5)
        me_eig = lax.axis_index("eig")

        def finish(piece):
            weights = piece[:samples].astype(jnp.bfloat16)
            sums = piece[samples:]
            high = sums.astype(jnp.bfloat16)
            low = (sums - high.astype(jnp.float32)).astype(jnp.bfloat16)
            return jnp.concatenate([weights, high, low], 0)

        def decode(block):
            return jnp.concatenate(
                [
                    block[:samples].astype(jnp.float32),
                    block[samples : samples + 8].astype(jnp.float32)
                    + block[samples + 8 :].astype(jnp.float32),
                ],
                0,
            )

        def operate(vector, first=False):
            lowered = vector.astype(jnp.bfloat16)
            if pair:
                rows = jnp.concatenate([lowered, lax.ppermute(lowered, "eig", swap)], 0)
            else:
                rows = lax.all_gather(lowered, "eig", axis=0, tiled=True)
            if first:
                coeff = coeff_from_table(rows)
            else:
                coeff = jnp.dot(rows, built[0], preferred_element_type=jnp.float32)
            sums = jnp.zeros((8, group), jnp.float32)
            sums = sums.at[0, :own].set(jnp.sum(vector * vector, axis=1))
            sums = sums.at[1, :own].set(jnp.sum(noise_var[None, :] * vector * vector, axis=1))
            gathered, side = vert_sum(
                jnp.concatenate([coeff * spectrum[None, :], sums], 0),
                n_vert,
                finish,
                finish,
                decode,
                [piece(p) for p in range(pieces)] if first else (),
            )
            if first:
                built.append(jnp.concatenate(side, 0))
            features = built[0]
            weights = gathered[:samples]
            sums = gathered[samples : samples + 8].astype(jnp.float32) + gathered[
                samples + 8 : samples + 16
            ].astype(jnp.float32)
            wide = weights.astype(jnp.float32)
            energy = jnp.sum(wide * wide / spectrum[None, :], axis=1)
            partials = lax.dot_general(
                weights, features, (((1,), (1,)), ((), ())), preferred_element_type=jnp.float32
            ).astype(jnp.bfloat16)
            if pair:
                energy = energy[:own] + lax.ppermute(energy[own:], "eig", swap)
                image = partials[:own].astype(jnp.float32) + lax.ppermute(
                    partials[own:], "eig", swap
                ).astype(jnp.float32)
            else:
                energy = lax.psum_scatter(energy, "eig", scatter_dimension=0, tiled=True)
                image = lax.psum_scatter(
                    partials, "eig", scatter_dimension=0, tiled=True
                ).astype(jnp.float32)
            image = jnp.where(filled[None, :], image, jnp.zeros((), jnp.float32))
            norm = sums[0, :own]
            product = sums[1, :own] + energy
            return image + noise_var[None, :] * vector, norm, product

        residual = jnp.where(filled[None, :], rhs, jnp.zeros((), jnp.float32))
        solution = jnp.zeros_like(residual)
        applied, norm_now, product = operate(residual, first=True)
        step_size = norm_now / product
        direction, along = (residual, applied)
        for iteration in range(ITERS):
            solution = solution + step_size[:, None] * direction
            residual = residual - step_size[:, None] * along
            if iteration + 1 < ITERS:
                applied, norm_next, product = operate(residual)
                beta_ratio = norm_next / norm_now
                step_size = norm_next / (product - beta_ratio * norm_next / step_size)
                direction = residual + beta_ratio[:, None] * direction
                along = applied + beta_ratio[:, None] * along
                norm_now = norm_next
        return (solution, residual)

    return shards


def solution(mesh):
    return jax.shard_map(
        make_shards(mesh.shape["vert"], mesh.shape["eig"]),
        mesh=mesh,
        in_specs=(P("vert", "eig"), P("vert"), P("vert"), P("vert"), P("eig"), P("eig", "vert")),
        out_specs=(P("eig", "vert"), P("eig", "vert")),
        check_vma=False,
    )
```

```python
import jax
import jax.numpy as jnp
from jax import lax
from jax.sharding import PartitionSpec as P

ITERS = 2
PIECES = 3


def vert_sum(x, n_vert, finish, encode, decode, side=()):
    side = list(side)

    def beside(k, sent, received):
        if k >= len(side):
            return received
        out = side[k](sent)
        received, out = lax.optimization_barrier((received, out))
        side[k] = out
        return received

    bits = n_vert.bit_length() - 1
    rounds = [list(range(b, min(b + 2, bits))) for b in range(0, bits, 2)]
    me = lax.axis_index("vert")
    cur = x
    plan = []
    for group in rounds:
        n = 1 << len(group)
        digit = sum(((me >> b) & 1) << i for i, b in enumerate(group))
        masks = [sum(((t >> i) & 1) << b for i, b in enumerate(group)) for t in range(n)]
        width = cur.shape[1] // n
        total = lax.dynamic_slice_in_dim(cur, digit * width, width, axis=1)
        sends = [
            encode(lax.dynamic_slice_in_dim(cur, (digit ^ t) * width, width, axis=1))
            for t in range(1, n)
        ]
        gots = [
            lax.ppermute(send, "vert", [(i, i ^ masks[t + 1]) for i in range(n_vert)])
            for t, send in enumerate(sends)
        ]
        gots = beside(len(plan), sends[0], gots)
        for got in gots:
            total = total + decode(got)
        cur = total
        plan.append((n, digit, masks))
    cur = finish(cur)
    for k, (n, digit, masks) in enumerate(reversed(plan), len(plan)):
        width = cur.shape[1]
        out = jnp.zeros((cur.shape[0], width * n), cur.dtype)
        out = lax.dynamic_update_slice_in_dim(out, cur, digit * width, axis=1)
        gots = [
            lax.ppermute(cur, "vert", [(i, i ^ masks[t]) for i in range(n_vert)]) for t in range(1, n)
        ]
        gots = beside(k, cur, gots)
        for t, got in enumerate(gots, 1):
            out = lax.dynamic_update_slice_in_dim(out, got, (digit ^ t) * width, axis=1)
        cur = out
    return cur, side


def make_shards(n_vert, n_eig):
    pair = n_eig == 2
    swap = [(0, 1), (1, 0)]

    def shards(eig_table, obs_ids, counts, noise_var, eigenvalues, rhs):
        capacity = obs_ids.shape[0]
        own = rhs.shape[0]
        samples = own * n_eig
        group = eig_table.shape[1]
        filled = jnp.arange(capacity, dtype=jnp.int32) < counts[0]
        vertices = jnp.arange(eig_table.shape[0], dtype=jnp.int32)
        picker = (obs_ids[:, None] == vertices[None, :]).astype(jnp.bfloat16)
        pieces = PIECES if capacity % (8 * PIECES) == 0 else 1
        span = capacity // pieces

        def piece(p):
            def work(anchor):
                ids, _ = lax.optimization_barrier((obs_ids[p * span : (p + 1) * span], anchor))
                rows = (ids[:, None] == vertices[None, :]).astype(jnp.bfloat16)
                return jnp.dot(rows, eig_table, preferred_element_type=jnp.float32).astype(jnp.bfloat16)

            return work

        built = []

        def coeff_from_table(rows):
            summed = jnp.dot(rows, picker, preferred_element_type=jnp.float32)
            high = summed.astype(jnp.bfloat16)
            low = (summed - high.astype(jnp.float32)).astype(jnp.bfloat16)
            both = jnp.dot(
                jnp.concatenate([high, low], 0), eig_table, preferred_element_type=jnp.float32
            )
            return both[: rows.shape[0]] + both[rows.shape[0] :]
        spectrum = 5.0 * jnp.power(3.0 + eigenvalues, -1.5)
        me_eig = lax.axis_index("eig")

        def finish(piece):
            weights = piece[:samples].astype(jnp.bfloat16)
            sums = piece[samples:]
            high = sums.astype(jnp.bfloat16)
            low = (sums - high.astype(jnp.float32)).astype(jnp.bfloat16)
            return jnp.concatenate([weights, high, low], 0)

        def decode(block):
            return jnp.concatenate(
                [
                    block[:samples].astype(jnp.float32),
                    block[samples : samples + 8].astype(jnp.float32)
                    + block[samples + 8 :].astype(jnp.float32),
                ],
                0,
            )

        def operate(vector, first=False):
            lowered = vector.astype(jnp.bfloat16)
            if pair:
                rows = jnp.concatenate([lowered, lax.ppermute(lowered, "eig", swap)], 0)
            else:
                rows = lax.all_gather(lowered, "eig", axis=0, tiled=True)
            if first:
                coeff = coeff_from_table(rows)
            else:
                coeff = sum(
                    jnp.dot(rows[:, a:b], built[p], preferred_element_type=jnp.float32)
                    for p, (a, b) in enumerate((p * span, (p + 1) * span) for p in range(pieces))
                )
            sums = jnp.zeros((8, group), jnp.float32)
            sums = sums.at[0, :own].set(jnp.sum(vector * vector, axis=1))
            sums = sums.at[1, :own].set(jnp.sum(noise_var[None, :] * vector * vector, axis=1))
            gathered, side = vert_sum(
                jnp.concatenate([coeff * spectrum[None, :], sums], 0),
                n_vert,
                finish,
                finish,
                decode,
                [piece(p) for p in range(pieces)] if first else (),
            )
            if first:
                built.extend(side)
            weights = gathered[:samples]
            sums = gathered[samples : samples + 8].astype(jnp.float32) + gathered[
                samples + 8 : samples + 16
            ].astype(jnp.float32)
            wide = weights.astype(jnp.float32)
            energy = jnp.sum(wide * wide / spectrum[None, :], axis=1)
            partials = jnp.concatenate(
                [
                    lax.dot_general(
                        weights, built[p], (((1,), (1,)), ((), ())), preferred_element_type=jnp.float32
                    ).astype(jnp.bfloat16)
                    for p in range(pieces)
                ],
                1,
            )
            if pair:
                energy = energy[:own] + lax.ppermute(energy[own:], "eig", swap)
                image = partials[:own].astype(jnp.float32) + lax.ppermute(
                    partials[own:], "eig", swap
                ).astype(jnp.float32)
            else:
                energy = lax.psum_scatter(energy, "eig", scatter_dimension=0, tiled=True)
                image = lax.psum_scatter(
                    partials, "eig", scatter_dimension=0, tiled=True
                ).astype(jnp.float32)
            image = jnp.where(filled[None, :], image, jnp.zeros((), jnp.float32))
            norm = sums[0, :own]
            product = sums[1, :own] + energy
            return image + noise_var[None, :] * vector, norm, product

        residual = jnp.where(filled[None, :], rhs, jnp.zeros((), jnp.float32))
        solution = jnp.zeros_like(residual)
        applied, norm_now, product = operate(residual, first=True)
        step_size = norm_now / product
        direction, along = (residual, applied)
        for iteration in range(ITERS):
            solution = solution + step_size[:, None] * direction
            residual = residual - step_size[:, None] * along
            if iteration + 1 < ITERS:
                applied, norm_next, product = operate(residual)
                beta_ratio = norm_next / norm_now
                step_size = norm_next / (product - beta_ratio * norm_next / step_size)
                direction = residual + beta_ratio[:, None] * direction
                along = applied + beta_ratio[:, None] * along
                norm_now = norm_next
        return (solution, residual)

    return shards


def solution(mesh):
    return jax.shard_map(
        make_shards(mesh.shape["vert"], mesh.shape["eig"]),
        mesh=mesh,
        in_specs=(P("vert", "eig"), P("vert"), P("vert"), P("vert"), P("eig"), P("eig", "vert")),
        out_specs=(P("eig", "vert"), P("eig", "vert")),
        check_vma=False,
    )
```

```python
import jax
import jax.numpy as jnp
from jax import lax
from jax.sharding import PartitionSpec as P

ITERS = 2
PIECES = 3


def vert_sum(x, n_vert, finish, encode, decode, side=()):
    side = list(side)

    def beside(k, sent, received):
        if k >= len(side):
            return received
        out = side[k](sent)
        received, out = lax.optimization_barrier((received, out))
        side[k] = out
        return received

    bits = n_vert.bit_length() - 1
    rounds = [list(range(b, min(b + 2, bits))) for b in range(0, bits, 2)]
    me = lax.axis_index("vert")
    cur = x
    plan = []
    for group in rounds:
        n = 1 << len(group)
        digit = sum(((me >> b) & 1) << i for i, b in enumerate(group))
        masks = [sum(((t >> i) & 1) << b for i, b in enumerate(group)) for t in range(n)]
        width = cur.shape[1] // n
        total = lax.dynamic_slice_in_dim(cur, digit * width, width, axis=1)
        sends = [
            encode(lax.dynamic_slice_in_dim(cur, (digit ^ t) * width, width, axis=1))
            for t in range(1, n)
        ]
        gots = [
            lax.ppermute(send, "vert", [(i, i ^ masks[t + 1]) for i in range(n_vert)])
            for t, send in enumerate(sends)
        ]
        gots = beside(len(plan), sends[0], gots)
        for got in gots:
            total = total + decode(got)
        cur = total
        plan.append((n, digit, masks))
    cur = finish(cur)
    for k, (n, digit, masks) in enumerate(reversed(plan), len(plan)):
        width = cur.shape[1]
        out = jnp.zeros((cur.shape[0], width * n), cur.dtype)
        out = lax.dynamic_update_slice_in_dim(out, cur, digit * width, axis=1)
        gots = [
            lax.ppermute(cur, "vert", [(i, i ^ masks[t]) for i in range(n_vert)]) for t in range(1, n)
        ]
        gots = beside(k, cur, gots)
        for t, got in enumerate(gots, 1):
            out = lax.dynamic_update_slice_in_dim(out, got, (digit ^ t) * width, axis=1)
        cur = out
    return cur, side


def make_shards(n_vert, n_eig):
    pair = n_eig == 2
    swap = [(0, 1), (1, 0)]

    def shards(eig_table, obs_ids, counts, noise_var, eigenvalues, rhs):
        capacity = obs_ids.shape[0]
        own = rhs.shape[0]
        samples = own * n_eig
        group = eig_table.shape[1]
        filled = jnp.arange(capacity, dtype=jnp.int32) < counts[0]
        vertices = jnp.arange(eig_table.shape[0], dtype=jnp.int32)
        picker = (obs_ids[:, None] == vertices[None, :]).astype(jnp.bfloat16)
        pieces = PIECES if capacity % (8 * PIECES) == 0 else 1
        span = capacity // pieces

        def piece(p):
            def work(anchor):
                ids, _ = lax.optimization_barrier((obs_ids[p * span : (p + 1) * span], anchor))
                rows = (ids[:, None] == vertices[None, :]).astype(jnp.bfloat16)
                return jnp.dot(rows, eig_table, preferred_element_type=jnp.float32).astype(jnp.bfloat16)

            return work

        built = []

        def coeff_from_table(rows):
            summed = jnp.dot(rows, picker, preferred_element_type=jnp.float32)
            high = summed.astype(jnp.bfloat16)
            low = (summed - high.astype(jnp.float32)).astype(jnp.bfloat16)
            both = jnp.dot(
                jnp.concatenate([high, low], 0), eig_table, preferred_element_type=jnp.float32
            )
            return both[: rows.shape[0]] + both[rows.shape[0] :]
        spectrum = 5.0 * jnp.power(3.0 + eigenvalues, -1.5)
        me_eig = lax.axis_index("eig")

        def finish(piece):
            weights = piece[:samples].astype(jnp.bfloat16)
            sums = piece[samples:]
            high = sums.astype(jnp.bfloat16)
            low = (sums - high.astype(jnp.float32)).astype(jnp.bfloat16)
            return jnp.concatenate([weights, high, low], 0)

        def decode(block):
            return jnp.concatenate(
                [
                    block[:samples].astype(jnp.float32),
                    block[samples : samples + 8].astype(jnp.float32)
                    + block[samples + 8 :].astype(jnp.float32),
                ],
                0,
            )

        def operate(vector, first=False):
            lowered = vector.astype(jnp.bfloat16)
            project = coeff_from_table if first else (
                lambda rows: jnp.dot(rows, built[0], preferred_element_type=jnp.float32)
            )
            if pair and not first:
                coeff = jnp.concatenate(
                    [project(lowered), project(lax.ppermute(lowered, "eig", swap))], 0
                )
            elif pair:
                coeff = project(jnp.concatenate([lowered, lax.ppermute(lowered, "eig", swap)], 0))
            else:
                coeff = project(lax.all_gather(lowered, "eig", axis=0, tiled=True))
            sums = jnp.zeros((8, group), jnp.float32)
            sums = sums.at[0, :own].set(jnp.sum(vector * vector, axis=1))
            sums = sums.at[1, :own].set(jnp.sum(noise_var[None, :] * vector * vector, axis=1))
            gathered, side = vert_sum(
                jnp.concatenate([coeff * spectrum[None, :], sums], 0),
                n_vert,
                finish,
                finish,
                decode,
                [piece(p) for p in range(pieces)] if first else (),
            )
            if first:
                built.append(jnp.concatenate(side, 0))
            features = built[0]
            weights = gathered[:samples]
            sums = gathered[samples : samples + 8].astype(jnp.float32) + gathered[
                samples + 8 : samples + 16
            ].astype(jnp.float32)
            wide = weights.astype(jnp.float32)
            energy = jnp.sum(wide * wide / spectrum[None, :], axis=1)
            def image_of(rows):
                return lax.dot_general(
                    rows, features, (((1,), (1,)), ((), ())), preferred_element_type=jnp.float32
                ).astype(jnp.bfloat16)

            if pair:
                energy = energy[:own] + lax.ppermute(energy[own:], "eig", swap)
                theirs = lax.ppermute(image_of(weights[own:]), "eig", swap)
                image = image_of(weights[:own]).astype(jnp.float32) + theirs.astype(jnp.float32)
            else:
                partials = image_of(weights)
                energy = lax.psum_scatter(energy, "eig", scatter_dimension=0, tiled=True)
                image = lax.psum_scatter(
                    partials, "eig", scatter_dimension=0, tiled=True
                ).astype(jnp.float32)
            image = jnp.where(filled[None, :], image, jnp.zeros((), jnp.float32))
            norm = sums[0, :own]
            product = sums[1, :own] + energy
            return image + noise_var[None, :] * vector, norm, product

        residual = jnp.where(filled[None, :], rhs, jnp.zeros((), jnp.float32))
        solution = jnp.zeros_like(residual)
        applied, norm_now, product = operate(residual, first=True)
        step_size = norm_now / product
        direction, along = (residual, applied)
        for iteration in range(ITERS):
            solution = solution + step_size[:, None] * direction
            residual = residual - step_size[:, None] * along
            if iteration + 1 < ITERS:
                applied, norm_next, product = operate(residual)
                beta_ratio = norm_next / norm_now
                step_size = norm_next / (product - beta_ratio * norm_next / step_size)
                direction = residual + beta_ratio[:, None] * direction
                along = applied + beta_ratio[:, None] * along
                norm_now = norm_next
        return (solution, residual)

    return shards


def solution(mesh):
    return jax.shard_map(
        make_shards(mesh.shape["vert"], mesh.shape["eig"]),
        mesh=mesh,
        in_specs=(P("vert", "eig"), P("vert"), P("vert"), P("vert"), P("eig"), P("eig", "vert")),
        out_specs=(P("eig", "vert"), P("eig", "vert")),
        check_vma=False,
    )
```

```python
import jax
import jax.numpy as jnp
from jax import lax
from jax.sharding import PartitionSpec as P

ITERS = 2
PIECES = 3


def vert_sum(x, n_vert, finish, encode, decode, side=()):
    side = list(side)

    def beside(k, sent, received):
        if k >= len(side):
            return received
        out = side[k](sent)
        received, out = lax.optimization_barrier((received, out))
        side[k] = out
        return received

    bits = n_vert.bit_length() - 1
    rounds = [list(range(b, min(b + 3, bits))) for b in range(0, bits, 3)]
    me = lax.axis_index("vert")
    cur = x
    plan = []
    for group in rounds:
        n = 1 << len(group)
        digit = sum(((me >> b) & 1) << i for i, b in enumerate(group))
        masks = [sum(((t >> i) & 1) << b for i, b in enumerate(group)) for t in range(n)]
        width = cur.shape[1] // n
        total = lax.dynamic_slice_in_dim(cur, digit * width, width, axis=1)
        sends = [
            encode(lax.dynamic_slice_in_dim(cur, (digit ^ t) * width, width, axis=1))
            for t in range(1, n)
        ]
        gots = [
            lax.ppermute(send, "vert", [(i, i ^ masks[t + 1]) for i in range(n_vert)])
            for t, send in enumerate(sends)
        ]
        gots = beside(len(plan), sends[0], gots)
        for got in gots:
            total = total + decode(got)
        cur = total
        plan.append((n, digit, masks))
    cur = finish(cur)
    for k, (n, digit, masks) in enumerate(reversed(plan), len(plan)):
        width = cur.shape[1]
        out = jnp.zeros((cur.shape[0], width * n), cur.dtype)
        out = lax.dynamic_update_slice_in_dim(out, cur, digit * width, axis=1)
        gots = [
            lax.ppermute(cur, "vert", [(i, i ^ masks[t]) for i in range(n_vert)]) for t in range(1, n)
        ]
        gots = beside(k, cur, gots)
        for t, got in enumerate(gots, 1):
            out = lax.dynamic_update_slice_in_dim(out, got, (digit ^ t) * width, axis=1)
        cur = out
    return cur, side


def make_shards(n_vert, n_eig):
    pair = n_eig == 2
    swap = [(0, 1), (1, 0)]

    def shards(eig_table, obs_ids, counts, noise_var, eigenvalues, rhs):
        capacity = obs_ids.shape[0]
        own = rhs.shape[0]
        samples = own * n_eig
        group = eig_table.shape[1]
        filled = jnp.arange(capacity, dtype=jnp.int32) < counts[0]
        vertices = jnp.arange(eig_table.shape[0], dtype=jnp.int32)
        picker = (obs_ids[:, None] == vertices[None, :]).astype(jnp.bfloat16)
        pieces = PIECES if capacity % (8 * PIECES) == 0 else 1
        span = capacity // pieces

        def piece(p):
            def work(anchor):
                ids, _ = lax.optimization_barrier((obs_ids[p * span : (p + 1) * span], anchor))
                rows = (ids[:, None] == vertices[None, :]).astype(jnp.bfloat16)
                return jnp.dot(rows, eig_table, preferred_element_type=jnp.float32).astype(jnp.bfloat16)

            return work

        built = []

        def coeff_from_table(rows):
            summed = jnp.dot(rows, picker, preferred_element_type=jnp.float32)
            high = summed.astype(jnp.bfloat16)
            low = (summed - high.astype(jnp.float32)).astype(jnp.bfloat16)
            both = jnp.dot(
                jnp.concatenate([high, low], 0), eig_table, preferred_element_type=jnp.float32
            )
            return both[: rows.shape[0]] + both[rows.shape[0] :]
        spectrum = 5.0 * jnp.power(3.0 + eigenvalues, -1.5)
        me_eig = lax.axis_index("eig")

        def finish(piece):
            weights = piece[:samples].astype(jnp.bfloat16)
            sums = piece[samples:]
            high = sums.astype(jnp.bfloat16)
            low = (sums - high.astype(jnp.float32)).astype(jnp.bfloat16)
            return jnp.concatenate([weights, high, low], 0)

        def decode(block):
            return jnp.concatenate(
                [
                    block[:samples].astype(jnp.float32),
                    block[samples : samples + 8].astype(jnp.float32)
                    + block[samples + 8 :].astype(jnp.float32),
                ],
                0,
            )

        def operate(vector, first=False):
            lowered = vector.astype(jnp.bfloat16)
            if pair:
                rows = jnp.concatenate([lowered, lax.ppermute(lowered, "eig", swap)], 0)
            else:
                rows = lax.all_gather(lowered, "eig", axis=0, tiled=True)
            if first:
                coeff = coeff_from_table(rows)
            else:
                coeff = jnp.dot(rows, built[0], preferred_element_type=jnp.float32)
            sums = jnp.zeros((8, group), jnp.float32)
            sums = sums.at[0, :own].set(jnp.sum(vector * vector, axis=1))
            sums = sums.at[1, :own].set(jnp.sum(noise_var[None, :] * vector * vector, axis=1))
            gathered, side = vert_sum(
                jnp.concatenate([coeff * spectrum[None, :], sums], 0),
                n_vert,
                finish,
                finish,
                decode,
                [piece(p) for p in range(pieces)] if first else (),
            )
            if first:
                built.append(jnp.concatenate(side, 0))
            features = built[0]
            weights = gathered[:samples]
            sums = gathered[samples : samples + 8].astype(jnp.float32) + gathered[
                samples + 8 : samples + 16
            ].astype(jnp.float32)
            wide = weights.astype(jnp.float32)
            energy = jnp.sum(wide * wide / spectrum[None, :], axis=1)
            partials = lax.dot_general(
                weights, features, (((1,), (1,)), ((), ())), preferred_element_type=jnp.float32
            ).astype(jnp.bfloat16)
            if pair:
                energy = energy[:own] + lax.ppermute(energy[own:], "eig", swap)
                image = partials[:own].astype(jnp.float32) + lax.ppermute(
                    partials[own:], "eig", swap
                ).astype(jnp.float32)
            else:
                energy = lax.psum_scatter(energy, "eig", scatter_dimension=0, tiled=True)
                image = lax.psum_scatter(
                    partials, "eig", scatter_dimension=0, tiled=True
                ).astype(jnp.float32)
            image = jnp.where(filled[None, :], image, jnp.zeros((), jnp.float32))
            norm = sums[0, :own]
            product = sums[1, :own] + energy
            return image + noise_var[None, :] * vector, norm, product

        residual = jnp.where(filled[None, :], rhs, jnp.zeros((), jnp.float32))
        solution = jnp.zeros_like(residual)
        applied, norm_now, product = operate(residual, first=True)
        step_size = norm_now / product
        direction, along = (residual, applied)
        for iteration in range(ITERS):
            solution = solution + step_size[:, None] * direction
            residual = residual - step_size[:, None] * along
            if iteration + 1 < ITERS:
                applied, norm_next, product = operate(residual)
                beta_ratio = norm_next / norm_now
                step_size = norm_next / (product - beta_ratio * norm_next / step_size)
                direction = residual + beta_ratio[:, None] * direction
                along = applied + beta_ratio[:, None] * along
                norm_now = norm_next
        return (solution, residual)

    return shards


def solution(mesh):
    return jax.shard_map(
        make_shards(mesh.shape["vert"], mesh.shape["eig"]),
        mesh=mesh,
        in_specs=(P("vert", "eig"), P("vert"), P("vert"), P("vert"), P("eig"), P("eig", "vert")),
        out_specs=(P("eig", "vert"), P("eig", "vert")),
        check_vma=False,
    )
```

```python
import jax
import jax.numpy as jnp
from jax import lax
from jax.sharding import PartitionSpec as P

ITERS = 2
PIECES = 3


def vert_sum(x, n_vert, finish, encode, decode, side=()):
    side = list(side)

    def beside(k, sent, received):
        if k >= len(side):
            return received
        out = side[k](sent)
        received, out = lax.optimization_barrier((received, out))
        side[k] = out
        return received

    bits = n_vert.bit_length() - 1
    rounds = [list(range(b, min(b + 2, bits))) for b in range(0, bits, 2)]
    me = lax.axis_index("vert")
    cur = x
    plan = []
    for group in rounds:
        n = 1 << len(group)
        digit = sum(((me >> b) & 1) << i for i, b in enumerate(group))
        masks = [sum(((t >> i) & 1) << b for i, b in enumerate(group)) for t in range(n)]
        width = cur.shape[1] // n
        total = lax.dynamic_slice_in_dim(cur, digit * width, width, axis=1)
        sends = [
            encode(lax.dynamic_slice_in_dim(cur, (digit ^ t) * width, width, axis=1))
            for t in range(1, n)
        ]
        gots = [
            lax.ppermute(send, "vert", [(i, i ^ masks[t + 1]) for i in range(n_vert)])
            for t, send in enumerate(sends)
        ]
        gots = beside(len(plan), sends[0], gots)
        for got in gots:
            total = total + decode(got)
        cur = total
        plan.append((n, digit, masks))
    cur = finish(cur)
    for k, (n, digit, masks) in enumerate(reversed(plan), len(plan)):
        width = cur.shape[1]
        out = jnp.zeros((cur.shape[0], width * n), cur.dtype)
        out = lax.dynamic_update_slice_in_dim(out, cur, digit * width, axis=1)
        gots = [
            lax.ppermute(cur, "vert", [(i, i ^ masks[t]) for i in range(n_vert)]) for t in range(1, n)
        ]
        gots = beside(k, cur, gots)
        for t, got in enumerate(gots, 1):
            out = lax.dynamic_update_slice_in_dim(out, got, (digit ^ t) * width, axis=1)
        cur = out
    return cur, side


def make_shards(n_vert, n_eig):
    pair = n_eig == 2
    swap = [(0, 1), (1, 0)]

    def shards(eig_table, obs_ids, counts, noise_var, eigenvalues, rhs):
        capacity = obs_ids.shape[0]
        own = rhs.shape[0]
        samples = own * n_eig
        group = eig_table.shape[1]
        filled = jnp.arange(capacity, dtype=jnp.int32) < counts[0]
        vertices = jnp.arange(eig_table.shape[0], dtype=jnp.int32)
        picker = (obs_ids[:, None] == vertices[None, :]).astype(jnp.bfloat16)
        pieces = PIECES if capacity % (8 * PIECES) == 0 else 1
        span = capacity // pieces

        def piece(p):
            def work(anchor):
                ids, _ = lax.optimization_barrier((obs_ids[p * span : (p + 1) * span], anchor))
                rows = (ids[:, None] == vertices[None, :]).astype(jnp.bfloat16)
                return jnp.dot(rows, eig_table, preferred_element_type=jnp.float32).astype(jnp.bfloat16)

            return work

        built = []

        def coeff_from_table(rows):
            summed = jnp.dot(rows, picker, preferred_element_type=jnp.float32)
            high = summed.astype(jnp.bfloat16)
            low = (summed - high.astype(jnp.float32)).astype(jnp.bfloat16)
            both = jnp.dot(
                jnp.concatenate([high, low], 0), eig_table, preferred_element_type=jnp.float32
            )
            return both[: rows.shape[0]] + both[rows.shape[0] :]
        spectrum = 5.0 * jnp.power(3.0 + eigenvalues, -1.5)
        me_eig = lax.axis_index("eig")

        def finish(piece):
            weights = piece[:samples].astype(jnp.bfloat16)
            sums = piece[samples:]
            high = sums.astype(jnp.bfloat16)
            low = (sums - high.astype(jnp.float32)).astype(jnp.bfloat16)
            return jnp.concatenate([weights, high, low], 0)

        def decode(block):
            return jnp.concatenate(
                [
                    block[:samples].astype(jnp.float32),
                    block[samples : samples + 8].astype(jnp.float32)
                    + block[samples + 8 :].astype(jnp.float32),
                ],
                0,
            )

        def operate(vector, first=False):
            lowered = vector.astype(jnp.bfloat16)
            if pair:
                arrived = lax.ppermute(lowered, "eig", swap)
                rows = jnp.concatenate([lowered, arrived], 0)
            else:
                rows = lax.all_gather(lowered, "eig", axis=0, tiled=True)
            if first:
                coeff = coeff_from_table(rows)
            elif pair:
                coeff = jnp.concatenate(
                    [
                        jnp.dot(lowered, built[0], preferred_element_type=jnp.float32),
                        jnp.dot(arrived, built[0], preferred_element_type=jnp.float32),
                    ],
                    0,
                )
            else:
                coeff = jnp.dot(rows, built[0], preferred_element_type=jnp.float32)
            sums = jnp.zeros((8, group), jnp.float32)
            sums = sums.at[0, :own].set(jnp.sum(vector * vector, axis=1))
            sums = sums.at[1, :own].set(jnp.sum(noise_var[None, :] * vector * vector, axis=1))
            gathered, side = vert_sum(
                jnp.concatenate([coeff * spectrum[None, :], sums], 0),
                n_vert,
                finish,
                finish,
                decode,
                [piece(p) for p in range(pieces)] if first else (),
            )
            if first:
                built.append(jnp.concatenate(side, 0))
            features = built[0]
            weights = gathered[:samples]
            sums = gathered[samples : samples + 8].astype(jnp.float32) + gathered[
                samples + 8 : samples + 16
            ].astype(jnp.float32)
            wide = weights.astype(jnp.float32)
            energy = jnp.sum(wide * wide / spectrum[None, :], axis=1)
            partials = lax.dot_general(
                weights, features, (((1,), (1,)), ((), ())), preferred_element_type=jnp.float32
            ).astype(jnp.bfloat16)
            if pair:
                energy = energy[:own] + lax.ppermute(energy[own:], "eig", swap)
                image = partials[:own].astype(jnp.float32) + lax.ppermute(
                    partials[own:], "eig", swap
                ).astype(jnp.float32)
            else:
                energy = lax.psum_scatter(energy, "eig", scatter_dimension=0, tiled=True)
                image = lax.psum_scatter(
                    partials, "eig", scatter_dimension=0, tiled=True
                ).astype(jnp.float32)
            image = jnp.where(filled[None, :], image, jnp.zeros((), jnp.float32))
            norm = sums[0, :own]
            product = sums[1, :own] + energy
            return image + noise_var[None, :] * vector, norm, product

        residual = jnp.where(filled[None, :], rhs, jnp.zeros((), jnp.float32))
        solution = jnp.zeros_like(residual)
        applied, norm_now, product = operate(residual, first=True)
        step_size = norm_now / product
        direction, along = (residual, applied)
        for iteration in range(ITERS):
            solution = solution + step_size[:, None] * direction
            residual = residual - step_size[:, None] * along
            if iteration + 1 < ITERS:
                applied, norm_next, product = operate(residual)
                beta_ratio = norm_next / norm_now
                step_size = norm_next / (product - beta_ratio * norm_next / step_size)
                direction = residual + beta_ratio[:, None] * direction
                along = applied + beta_ratio[:, None] * along
                norm_now = norm_next
        return (solution, residual)

    return shards


def solution(mesh):
    return jax.shard_map(
        make_shards(mesh.shape["vert"], mesh.shape["eig"]),
        mesh=mesh,
        in_specs=(P("vert", "eig"), P("vert"), P("vert"), P("vert"), P("eig"), P("eig", "vert")),
        out_specs=(P("eig", "vert"), P("eig", "vert")),
        check_vma=False,
    )
```

```python
import jax
import jax.numpy as jnp
from jax import lax
from jax.sharding import PartitionSpec as P

ITERS = 2
PIECES = 3


def vert_sum(x, n_vert, finish, encode, decode, side=()):
    side = list(side)

    def beside(k, sent, received):
        if k >= len(side):
            return received
        out = side[k](sent)
        received, out = lax.optimization_barrier((received, out))
        side[k] = out
        return received

    bits = n_vert.bit_length() - 1
    rounds = [list(range(b, min(b + 2, bits))) for b in range(0, bits, 2)]
    me = lax.axis_index("vert")
    cur = x
    plan = []
    for group in rounds:
        n = 1 << len(group)
        digit = sum(((me >> b) & 1) << i for i, b in enumerate(group))
        masks = [sum(((t >> i) & 1) << b for i, b in enumerate(group)) for t in range(n)]
        width = cur.shape[1] // n
        total = lax.dynamic_slice_in_dim(cur, digit * width, width, axis=1)
        sends = [
            encode(lax.dynamic_slice_in_dim(cur, (digit ^ t) * width, width, axis=1))
            for t in range(1, n)
        ]
        gots = [
            lax.ppermute(send, "vert", [(i, i ^ masks[t + 1]) for i in range(n_vert)])
            for t, send in enumerate(sends)
        ]
        gots = beside(len(plan), sends[0], gots)
        for got in gots:
            total = total + decode(got)
        cur = total
        plan.append((n, digit, masks))
    cur = finish(cur)
    for k, (n, digit, masks) in enumerate(reversed(plan), len(plan)):
        width = cur.shape[1]
        out = jnp.zeros((cur.shape[0], width * n), cur.dtype)
        out = lax.dynamic_update_slice_in_dim(out, cur, digit * width, axis=1)
        gots = [
            lax.ppermute(cur, "vert", [(i, i ^ masks[t]) for i in range(n_vert)]) for t in range(1, n)
        ]
        gots = beside(k, cur, gots)
        for t, got in enumerate(gots, 1):
            out = lax.dynamic_update_slice_in_dim(out, got, (digit ^ t) * width, axis=1)
        cur = out
    return cur, side


def make_shards(n_vert, n_eig):
    pair = n_eig == 2
    swap = [(0, 1), (1, 0)]

    def shards(eig_table, obs_ids, counts, noise_var, eigenvalues, rhs):
        capacity = obs_ids.shape[0]
        own = rhs.shape[0]
        samples = own * n_eig
        group = eig_table.shape[1]
        filled = jnp.arange(capacity, dtype=jnp.int32) < counts[0]
        vertices = jnp.arange(eig_table.shape[0], dtype=jnp.int32)
        picker = (obs_ids[:, None] == vertices[None, :]).astype(jnp.bfloat16)
        pieces = PIECES if capacity % (8 * PIECES) == 0 else 1
        span = capacity // pieces

        def piece(p):
            def work(anchor):
                ids, _ = lax.optimization_barrier((obs_ids[p * span : (p + 1) * span], anchor))
                rows = (ids[:, None] == vertices[None, :]).astype(jnp.bfloat16)
                return jnp.dot(rows, eig_table, preferred_element_type=jnp.float32).astype(jnp.bfloat16)

            return work

        built = []

        def coeff_from_table(rows):
            summed = jnp.dot(rows, picker, preferred_element_type=jnp.float32)
            high = summed.astype(jnp.bfloat16)
            low = (summed - high.astype(jnp.float32)).astype(jnp.bfloat16)
            both = jnp.dot(
                jnp.concatenate([high, low], 0), eig_table, preferred_element_type=jnp.float32
            )
            return both[: rows.shape[0]] + both[rows.shape[0] :]
        spectrum = 5.0 * jnp.power(3.0 + eigenvalues, -1.5)
        me_eig = lax.axis_index("eig")

        def finish(piece):
            weights = piece[:samples].astype(jnp.bfloat16)
            sums = piece[samples:]
            high = sums.astype(jnp.bfloat16)
            low = (sums - high.astype(jnp.float32)).astype(jnp.bfloat16)
            return jnp.concatenate([weights, high, low], 0)

        def decode(block):
            return jnp.concatenate(
                [
                    block[:samples].astype(jnp.float32),
                    block[samples : samples + 8].astype(jnp.float32)
                    + block[samples + 8 :].astype(jnp.float32),
                ],
                0,
            )

        def operate(vector, first=False):
            lowered = vector.astype(jnp.bfloat16)
            if pair:
                rows = jnp.concatenate([lowered, lax.ppermute(lowered, "eig", swap)], 0)
            else:
                rows = lax.all_gather(lowered, "eig", axis=0, tiled=True)
            if first:
                coeff = coeff_from_table(rows)
            else:
                coeff = jnp.dot(rows, built[0], preferred_element_type=jnp.float32)
            sums = jnp.zeros((8, group), jnp.float32)
            sums = sums.at[0, :own].set(jnp.sum(vector * vector, axis=1))
            sums = sums.at[1, :own].set(jnp.sum(noise_var[None, :] * vector * vector, axis=1))
            gathered, side = vert_sum(
                jnp.concatenate([coeff * spectrum[None, :], sums], 0),
                n_vert,
                finish,
                finish,
                decode,
                [piece(p) for p in range(pieces)] if first else (),
            )
            if first:
                built.append(jnp.concatenate(side, 0))
            features = built[0]
            weights = gathered[:samples]
            sums = gathered[samples : samples + 8].astype(jnp.float32) + gathered[
                samples + 8 : samples + 16
            ].astype(jnp.float32)
            wide = weights.astype(jnp.float32)
            energy = jnp.sum(wide * wide / spectrum[None, :], axis=1)
            def image_of(rows):
                return lax.dot_general(
                    rows, features, (((1,), (1,)), ((), ())), preferred_element_type=jnp.float32
                ).astype(jnp.bfloat16)

            partials = image_of(weights)
            if pair and not first:
                energy = energy[:own] + lax.ppermute(energy[own:], "eig", swap)
                theirs = lax.ppermute(image_of(weights[own:]), "eig", swap)
                image = image_of(weights[:own]).astype(jnp.float32) + theirs.astype(jnp.float32)
            elif pair:
                energy = energy[:own] + lax.ppermute(energy[own:], "eig", swap)
                image = partials[:own].astype(jnp.float32) + lax.ppermute(
                    partials[own:], "eig", swap
                ).astype(jnp.float32)
            else:
                energy = lax.psum_scatter(energy, "eig", scatter_dimension=0, tiled=True)
                image = lax.psum_scatter(
                    partials, "eig", scatter_dimension=0, tiled=True
                ).astype(jnp.float32)
            image = jnp.where(filled[None, :], image, jnp.zeros((), jnp.float32))
            norm = sums[0, :own]
            product = sums[1, :own] + energy
            return image + noise_var[None, :] * vector, norm, product

        residual = jnp.where(filled[None, :], rhs, jnp.zeros((), jnp.float32))
        solution = jnp.zeros_like(residual)
        applied, norm_now, product = operate(residual, first=True)
        step_size = norm_now / product
        direction, along = (residual, applied)
        for iteration in range(ITERS):
            solution = solution + step_size[:, None] * direction
            residual = residual - step_size[:, None] * along
            if iteration + 1 < ITERS:
                applied, norm_next, product = operate(residual)
                beta_ratio = norm_next / norm_now
                step_size = norm_next / (product - beta_ratio * norm_next / step_size)
                direction = residual + beta_ratio[:, None] * direction
                along = applied + beta_ratio[:, None] * along
                norm_now = norm_next
        return (solution, residual)

    return shards


def solution(mesh):
    return jax.shard_map(
        make_shards(mesh.shape["vert"], mesh.shape["eig"]),
        mesh=mesh,
        in_specs=(P("vert", "eig"), P("vert"), P("vert"), P("vert"), P("eig"), P("eig", "vert")),
        out_specs=(P("eig", "vert"), P("eig", "vert")),
        check_vma=False,
    )
```

```python
import jax
import jax.numpy as jnp
from jax import lax
from jax.sharding import PartitionSpec as P

ITERS = 2
PIECES = 3


def vert_sum(x, n_vert, finish, encode, decode, side=()):
    side = list(side)

    def beside(k, sent, received):
        if k >= len(side):
            return received
        out = side[k](sent)
        received, out = lax.optimization_barrier((received, out))
        side[k] = out
        return received

    bits = n_vert.bit_length() - 1
    rounds = [list(range(b, min(b + 2, bits))) for b in range(0, bits, 2)]
    me = lax.axis_index("vert")
    cur = x
    plan = []
    for group in rounds:
        n = 1 << len(group)
        digit = sum(((me >> b) & 1) << i for i, b in enumerate(group))
        masks = [sum(((t >> i) & 1) << b for i, b in enumerate(group)) for t in range(n)]
        width = cur.shape[1] // n
        total = lax.dynamic_slice_in_dim(cur, digit * width, width, axis=1)
        sends = [
            encode(lax.dynamic_slice_in_dim(cur, (digit ^ t) * width, width, axis=1))
            for t in range(1, n)
        ]
        gots = [
            lax.ppermute(send, "vert", [(i, i ^ masks[t + 1]) for i in range(n_vert)])
            for t, send in enumerate(sends)
        ]
        gots = beside(len(plan), sends[0], gots)
        for got in gots:
            total = total + decode(got)
        cur = total
        plan.append((n, digit, masks))
    cur = finish(cur)
    for k, (n, digit, masks) in enumerate(reversed(plan), len(plan)):
        width = cur.shape[1]
        out = jnp.zeros((cur.shape[0], width * n), cur.dtype)
        out = lax.dynamic_update_slice_in_dim(out, cur, digit * width, axis=1)
        gots = [
            lax.ppermute(cur, "vert", [(i, i ^ masks[t]) for i in range(n_vert)]) for t in range(1, n)
        ]
        gots = beside(k, cur, gots)
        for t, got in enumerate(gots, 1):
            out = lax.dynamic_update_slice_in_dim(out, got, (digit ^ t) * width, axis=1)
        cur = out
    return cur, side


def make_shards(n_vert, n_eig):
    pair = n_eig == 2
    swap = [(0, 1), (1, 0)]

    def shards(eig_table, obs_ids, counts, noise_var, eigenvalues, rhs):
        capacity = obs_ids.shape[0]
        own = rhs.shape[0]
        samples = own * n_eig
        group = eig_table.shape[1]
        filled = jnp.arange(capacity, dtype=jnp.int32) < counts[0]
        vertices = jnp.arange(eig_table.shape[0], dtype=jnp.int32)
        picker = (obs_ids[:, None] == vertices[None, :]).astype(jnp.bfloat16)
        pieces = PIECES if capacity % (8 * PIECES) == 0 else 1
        span = capacity // pieces

        def piece(p):
            def work(anchor):
                ids, _ = lax.optimization_barrier((obs_ids[p * span : (p + 1) * span], anchor))
                rows = (ids[:, None] == vertices[None, :]).astype(jnp.bfloat16)
                return jnp.dot(rows, eig_table, preferred_element_type=jnp.float32).astype(jnp.bfloat16)

            return work

        built = []

        def coeff_from_table(rows):
            summed = jnp.dot(rows, picker, preferred_element_type=jnp.float32)
            high = summed.astype(jnp.bfloat16)
            low = (summed - high.astype(jnp.float32)).astype(jnp.bfloat16)
            both = jnp.dot(
                jnp.concatenate([high, low], 0), eig_table, preferred_element_type=jnp.float32
            )
            return both[: rows.shape[0]] + both[rows.shape[0] :]
        spectrum = 5.0 * jnp.power(3.0 + eigenvalues, -1.5)
        me_eig = lax.axis_index("eig")

        def finish(piece):
            weights = piece[:samples].astype(jnp.bfloat16)
            sums = piece[samples:]
            high = sums.astype(jnp.bfloat16)
            low = (sums - high.astype(jnp.float32)).astype(jnp.bfloat16)
            return jnp.concatenate([weights, high, low], 0)

        def decode(block):
            return jnp.concatenate(
                [
                    block[:samples].astype(jnp.float32),
                    block[samples : samples + 8].astype(jnp.float32)
                    + block[samples + 8 :].astype(jnp.float32),
                ],
                0,
            )

        def operate(vector, first=False):
            lowered = vector.astype(jnp.bfloat16)
            if pair:
                rows = jnp.concatenate([lowered, lax.ppermute(lowered, "eig", swap)], 0)
            else:
                rows = lax.all_gather(lowered, "eig", axis=0, tiled=True)
            if first:
                coeff = coeff_from_table(rows)
            else:
                coeff = jnp.dot(rows, built[0], preferred_element_type=jnp.float32)
            sums = jnp.zeros((8, group), jnp.float32)
            sums = sums.at[0, :own].set(jnp.sum(vector * vector, axis=1))
            sums = sums.at[1, :own].set(jnp.sum(noise_var[None, :] * vector * vector, axis=1))
            gathered, side = vert_sum(
                jnp.concatenate([coeff * spectrum[None, :], sums], 0),
                n_vert,
                finish,
                finish,
                decode,
                [piece(p) for p in range(pieces)] if first else (),
            )
            if first:
                built.append(jnp.concatenate(side, 0))
            features = built[0]
            weights = gathered[:samples]
            sums = gathered[samples : samples + 8].astype(jnp.float32) + gathered[
                samples + 8 : samples + 16
            ].astype(jnp.float32)
            wide = weights.astype(jnp.float32)
            energy = jnp.sum(wide * wide / spectrum[None, :], axis=1)
            partials = lax.dot_general(
                weights, features, (((1,), (1,)), ((), ())), preferred_element_type=jnp.float32
            ).astype(jnp.bfloat16)
            if pair:
                high = energy[own:].astype(jnp.bfloat16)
                low = (energy[own:] - high.astype(jnp.float32)).astype(jnp.bfloat16)
                extra = jnp.zeros((16, capacity), jnp.bfloat16).at[0, :own].set(high).at[1, :own].set(low)
                got = lax.ppermute(jnp.concatenate([partials[own:], extra], 0), "eig", swap)
                energy = energy[:own] + (
                    got[own, :own].astype(jnp.float32) + got[own + 1, :own].astype(jnp.float32)
                )
                image = partials[:own].astype(jnp.float32) + got[:own].astype(jnp.float32)
            else:
                energy = lax.psum_scatter(energy, "eig", scatter_dimension=0, tiled=True)
                image = lax.psum_scatter(
                    partials, "eig", scatter_dimension=0, tiled=True
                ).astype(jnp.float32)
            image = jnp.where(filled[None, :], image, jnp.zeros((), jnp.float32))
            norm = sums[0, :own]
            product = sums[1, :own] + energy
            return image + noise_var[None, :] * vector, norm, product

        residual = jnp.where(filled[None, :], rhs, jnp.zeros((), jnp.float32))
        solution = jnp.zeros_like(residual)
        applied, norm_now, product = operate(residual, first=True)
        step_size = norm_now / product
        direction, along = (residual, applied)
        for iteration in range(ITERS):
            solution = solution + step_size[:, None] * direction
            residual = residual - step_size[:, None] * along
            if iteration + 1 < ITERS:
                applied, norm_next, product = operate(residual)
                beta_ratio = norm_next / norm_now
                step_size = norm_next / (product - beta_ratio * norm_next / step_size)
                direction = residual + beta_ratio[:, None] * direction
                along = applied + beta_ratio[:, None] * along
                norm_now = norm_next
        return (solution, residual)

    return shards


def solution(mesh):
    return jax.shard_map(
        make_shards(mesh.shape["vert"], mesh.shape["eig"]),
        mesh=mesh,
        in_specs=(P("vert", "eig"), P("vert"), P("vert"), P("vert"), P("eig"), P("eig", "vert")),
        out_specs=(P("eig", "vert"), P("eig", "vert")),
        check_vma=False,
    )
```
